256 devices in a mesh: dp: 32 (over y, z_hi, core), tensor: 8 (over z_lo, x).
Axes of the slice: x: 4, y: 4, z: 8 (z_hi: 4, z_lo: 2; z = z_hi * 2 + z_lo), core: 2. Of those that a mesh axis runs over, the one named last changes fastest.
Arguments:
- inputs: bfloat16 [32768, 2048], P(('dp', 'tensor')), may hold values from -6 to 6
- norm_gain: float32 [2048], replicated, may hold values from 0.1 to 1.9
- proj_weight: bfloat16 [2048, 3, 2048], P('dp', None, 'tensor'), may hold values from -0.125 to 0.125
- filters: float32 [3, 7, 2048], P(None, None, 'tensor'), may hold values from -2.4 to 2.4
- cotangent: bfloat16 [32768, 2048], P('dp', 'tensor'), may hold values from -18 to 18
Outputs:
- mixed: bfloat16 [32768, 2048], P('dp', 'tensor')
- grad_inputs: bfloat16 [32768, 2048], P(('dp', 'tensor'))
- grad_proj: bfloat16 [2048, 3, 2048], P('dp', None, 'tensor')
- grad_filters: float32 [3, 7, 2048], P(None, None, 'tensor')
- grad_gain: float32 [2048], replicated
The draws below stay inside these ranges and needn't reach their ends.
All inputs are finite; a program needn't handle non-finite values.
Results may differ from the reference program's by a relative error of at most 0.02.
Values may be sent and summed in bfloat16 or wider, within the bound.
No kernel may reach another device: no remote copies, remote signals or barrier semaphores. Data moves between devices by JAX's collectives and lax.ppermute only.
A program may use at most 64 MiB of HBM per device.

```python
import math
import jax
import jax.numpy as jnp
from jax import lax

D = 2048
KW = 7
TOK_DEV = 1024
ROWS = 32768
N_DP = 32
N_TENSOR = 8


def draw_cotangent(key, part):
    position = jnp.arange(ROWS, dtype=jnp.float32) / max(ROWS - 1, 1)
    factor = jnp.exp(math.log(3.0) * position)[:, None]
    base = jax.random.truncated_normal(key, -6.0, 6.0, (ROWS, D), jnp.float32)
    return (base * factor).astype(jnp.bfloat16)


def levels(key, extent, shards, least, high):
    def one(dim, shards_of):
        heights = jax.random.uniform(jax.random.fold_in(jax.random.fold_in(key, 6), dim), (shards_of,), jnp.float32, least / len(shards), high / len(shards))
        return jnp.repeat(jnp.exp(heights), extent[dim] // shards_of).reshape((-1,) + (1,) * (len(extent) - dim - 1))

    level = one(*shards[0])
    for cut in shards[1:]:
        level = level * one(*cut)
    return level


def scatter_about(rng, shape, deviation, limit, shards=(), held_as=jnp.bfloat16):
    drawn = jax.random.normal(rng, shape, jnp.float32) * deviation
    if len(shards) > 0:
        drawn = levels(rng, shape, shards, -0.22, 0.18) * drawn
    return jnp.clip(drawn, min=-limit, max=limit).astype(held_as)


def setup_inputs(seed: int = 0) -> dict:
    arg_keys = jax.random.split(jax.random.key(seed), 6)
    return {
        "inputs": scatter_about(arg_keys[0], (ROWS, D), 1.0, 6.0, ((0, 256),)),
        "norm_gain": jnp.clip(1.0 + 0.18 * jax.random.normal(arg_keys[1], (D,), jnp.float32), 0.1, 1.9),
        "proj_weight": scatter_about(arg_keys[2], (D, 3, D), D ** -0.5, 0.125, ((0, 32), (2, 8))),
        "filters": scatter_about(arg_keys[3], (3, KW, D), 0.4, 2.4, ((2, 8),), jnp.float32),
        "cotangent": draw_cotangent(jax.random.fold_in(arg_keys[5], 71), 0),
    }


def reference(inputs, norm_gain, proj_weight, filters, cotangent):
    width = KW - 1
    wide = inputs.astype(jnp.float32)
    inv_rms = lax.rsqrt(lax.optimization_barrier(jnp.mean(wide * wide, axis=1, keepdims=True)) + 1e-05)
    normed = (wide * inv_rms * norm_gain).astype(jnp.bfloat16)
    streams = jnp.dot(normed, proj_weight.reshape(D, 3 * D), preferred_element_type=jnp.float32)
    streams = streams.reshape(ROWS, 3, D).astype(jnp.bfloat16)
    padded = jnp.concatenate([jnp.zeros((width, 3, D), jnp.bfloat16), streams], axis=0).astype(jnp.float32)
    conv = jnp.zeros((ROWS, 3, D), jnp.float32)
    for tap in range(KW):
        conv = conv + filters[:, tap, :] * padded[width - tap:width - tap + ROWS]
    mixed = (conv[:, 0] * conv[:, 1] * conv[:, 2]).astype(jnp.bfloat16)
    grad_out = cotangent.astype(jnp.float32)
    grad_conv = jnp.stack([grad_out * conv[:, 1] * conv[:, 2], grad_out * conv[:, 0] * conv[:, 2], grad_out * conv[:, 0] * conv[:, 1]], axis=1)
    grad_pad = jnp.concatenate([grad_conv, jnp.zeros((width, 3, D), jnp.float32)], axis=0)
    grad_acc = jnp.zeros((ROWS, 3, D), jnp.float32)
    for tap in range(KW):
        grad_acc = grad_acc + filters[:, tap, :] * grad_pad[tap:tap + ROWS]
    grad_streams = grad_acc.astype(jnp.bfloat16)
    grad_filters = jnp.stack([lax.optimization_barrier(jnp.sum(grad_conv * padded[width - tap:width - tap + ROWS], axis=0)) for tap in range(KW)], axis=1)
    block_normed = normed.reshape(N_DP, TOK_DEV, D)
    block_grads = grad_streams.reshape(N_DP, TOK_DEV, 3 * D)

    def add_block(total, pair):
        partial_sum = jnp.dot(pair[0].T, pair[1], preferred_element_type=jnp.float32)
        rounded = lax.optimization_barrier(partial_sum.astype(jnp.bfloat16))
        return (total + rounded.astype(jnp.float32), None)
    grad_total, _ = lax.scan(add_block, jnp.zeros((D, 3 * D), jnp.float32), (block_normed, block_grads))
    grad_proj = grad_total.reshape(D, 3, D).astype(jnp.bfloat16)
    group = D // N_TENSOR
    grad_normed = jnp.zeros((ROWS, D), jnp.float32)
    for member in range(N_TENSOR):
        grad_part = grad_streams[:, :, member * group:(member + 1) * group].reshape(ROWS, 3 * group)
        weight_part = proj_weight[:, :, member * group:(member + 1) * group].reshape(D, 3 * group)
        partial_sum = jnp.dot(grad_part, weight_part.T, preferred_element_type=jnp.float32)
        rounded = lax.optimization_barrier(partial_sum.astype(jnp.bfloat16))
        grad_normed = grad_normed + rounded.astype(jnp.float32)
    scaled = norm_gain * grad_normed
    grad_inputs = inv_rms * (scaled - wide * inv_rms * inv_rms * lax.optimization_barrier(jnp.mean(scaled * wide, axis=1, keepdims=True)))
    grad_gain = lax.optimization_barrier(jnp.sum(grad_normed * wide * inv_rms, axis=0))
    return (mixed, grad_inputs.astype(jnp.bfloat16), grad_proj, grad_filters, grad_gain)
```

```python
import jax
import jax.numpy as jnp
from jax import lax
from jax.sharding import PartitionSpec as P


def passed_along(shard, axis, by):
    size = lax.axis_size(axis)
    pairs = [(i, i + by) for i in range(size) if 0 <= i + by < size]
    return lax.ppermute(shard, axis, pairs)


def butterfly_sum(value, axis):
    size = lax.axis_size(axis)
    step = 1
    while step < size:
        pairs = [(i, i ^ step) for i in range(size)]
        value = value + lax.ppermute(value, axis, pairs)
        step *= 2
    return value


def body(inputs, norm_gain, proj_weight, filters, cotangent):
    taps = filters.shape[1]
    width = taps - 1
    rows = inputs.shape[0]
    wide = inputs.astype(jnp.float32)
    inv_rms = lax.rsqrt(jnp.mean(wide * wide, axis=1, keepdims=True) + 1e-05)
    weights = lax.all_gather(proj_weight, "dp", axis=0, tiled=True)
    gathered = lax.all_gather(inputs, "tensor", axis=0, tiled=True)
    wide_all = gathered.astype(jnp.float32)
    inv_all = lax.rsqrt(jnp.mean(wide_all * wide_all, axis=1, keepdims=True) + 1e-05)
    unit_all = wide_all * inv_all
    positions = (unit_all * norm_gain).astype(jnp.bfloat16)
    length = positions.shape[0]
    streams = jnp.einsum(
        "td,dsc->tsc", positions, weights, preferred_element_type=jnp.float32
    ).astype(jnp.bfloat16)
    before = passed_along(streams[length - width :], "dp", 1)
    extended = jnp.concatenate([before, streams], axis=0).astype(jnp.float32)
    conv = jnp.zeros(streams.shape, jnp.float32)
    for tap in range(taps):
        conv = conv + filters[:, tap, :] * extended[width - tap : width - tap + length]
    mixed = (conv[:, 0] * conv[:, 1] * conv[:, 2]).astype(jnp.bfloat16)
    grad_out = cotangent.astype(jnp.float32)
    grad_conv = jnp.stack(
        [
            grad_out * conv[:, 1] * conv[:, 2],
            grad_out * conv[:, 0] * conv[:, 2],
            grad_out * conv[:, 0] * conv[:, 1],
        ],
        axis=1,
    )
    after = passed_along(grad_conv[:width], "dp", -1)
    grad_extended = jnp.concatenate([grad_conv, after], axis=0)
    grad_acc = jnp.zeros(streams.shape, jnp.float32)
    for tap in range(taps):
        grad_acc = grad_acc + filters[:, tap, :] * grad_extended[tap : tap + length]
    grad_streams = grad_acc.astype(jnp.bfloat16)
    filter_local = jnp.stack(
        [
            jnp.sum(grad_conv * extended[width - tap : width - tap + length], axis=0)
            for tap in range(taps)
        ],
        axis=1,
    )
    grad_filters = butterfly_sum(filter_local, "dp")
    normed_terms = jnp.einsum(
        "tsc,dsc->td", grad_streams, weights, preferred_element_type=jnp.float32
    ).astype(jnp.bfloat16)
    gain_local = jnp.sum(normed_terms.astype(jnp.float32) * unit_all, axis=0)
    grad_normed = lax.psum_scatter(
        normed_terms, "tensor", scatter_dimension=0, tiled=True
    ).astype(jnp.float32)
    weight_terms = jnp.einsum(
        "td,tsc->dsc", positions, grad_streams, preferred_element_type=jnp.float32
    )
    grad_proj = lax.psum_scatter(
        weight_terms.astype(jnp.bfloat16), "dp", scatter_dimension=0, tiled=True
    )
    grad_gain = butterfly_sum(butterfly_sum(gain_local, "dp"), "tensor")
    scaled = norm_gain * grad_normed
    grad_inputs = inv_rms * (
        scaled - wide * inv_rms * inv_rms * jnp.mean(scaled * wide, axis=1, keepdims=True)
    )
    return (mixed, grad_inputs.astype(jnp.bfloat16), grad_proj, grad_filters, grad_gain)


def solution(mesh):
    return jax.shard_map(
        body,
        mesh=mesh,
        in_specs=(
            P(("dp", "tensor"), None),
            P(),
            P("dp", None, "tensor"),
            P(None, None, "tensor"),
            P("dp", "tensor"),
        ),
        out_specs=(
            P("dp", "tensor"),
            P(("dp", "tensor"), None),
            P("dp", None, "tensor"),
            P(None, None, "tensor"),
            P(),
        ),
        check_vma=False,
    )
```

```python
import jax
import jax.numpy as jnp
from jax import lax
from jax.sharding import PartitionSpec as P

RING = 4


def passed_along(shard, axis, by):
    size = lax.axis_size(axis)
    pairs = [(i, i + by) for i in range(size) if 0 <= i + by < size]
    return lax.ppermute(shard, axis, pairs)


def butterfly_sum(value, axis):
    size = lax.axis_size(axis)
    step = 1
    while step < size:
        pairs = [(i, i ^ step) for i in range(size)]
        value = value + lax.ppermute(value, axis, pairs)
        step *= 2
    return value


def along_x(value, by):
    size = lax.axis_size("tensor")
    pairs = [(i, (i // RING) * RING + (i % RING + by) % RING) for i in range(size)]
    return lax.ppermute(value, "tensor", pairs)


def across_z(value):
    size = lax.axis_size("tensor")
    pairs = [(i, (i + RING) % size) for i in range(size)]
    return lax.ppermute(value, "tensor", pairs)


def relative_slots():
    me = lax.axis_index("tensor")
    z, x = me // RING, me % RING
    r = jnp.arange(2 * RING, dtype=jnp.int32)
    dz, dx = r // RING, r % RING
    absolute = ((z + dz) % 2) * RING + (x + dx) % RING
    zs, xs = r // RING, r % RING
    relative = ((zs + z) % 2) * RING + (xs - x) % RING
    return absolute, relative


def gather_tensor(own):
    half = own.shape[0] // 2
    partner = across_z(own)
    from_left = along_x(own, 1)
    from_right = along_x(own, -1)
    partner_left = along_x(partner, 1)
    partner_right = along_x(partner, -1)
    far = jnp.concatenate(
        [along_x(from_left[:half], 1), along_x(from_right[half:], -1)], axis=0
    )
    partner_far = jnp.concatenate(
        [along_x(partner_left[:half], 1), along_x(partner_right[half:], -1)], axis=0
    )
    return jnp.stack(
        [own, from_right, far, from_left, partner, partner_right, partner_far, partner_left]
    )


def scatter_tensor(blocks):
    half = blocks.shape[1] // 2
    wide = blocks.astype(jnp.float32)
    shard = [wide[dx :: RING] for dx in range(RING)]
    got_left = along_x(blocks[2::RING, :half], 1)
    got_right = along_x(blocks[2::RING, half:], -1)
    send_right = jnp.concatenate(
        [shard[1][:, :half] + got_left.astype(jnp.float32), shard[1][:, half:]], axis=1
    )
    send_left = jnp.concatenate(
        [shard[3][:, :half], shard[3][:, half:] + got_right.astype(jnp.float32)], axis=1
    )
    column = (
        shard[0]
        + along_x(send_right.astype(jnp.bfloat16), 1).astype(jnp.float32)
        + along_x(send_left.astype(jnp.bfloat16), -1).astype(jnp.float32)
    )
    return column[0] + across_z(column[1].astype(jnp.bfloat16)).astype(jnp.float32)


def body(inputs, norm_gain, proj_weight, filters, cotangent):
    taps = filters.shape[1]
    width = taps - 1
    rows = inputs.shape[0]
    absolute, relative = relative_slots()
    wide = inputs.astype(jnp.float32)
    inv_rms = lax.rsqrt(jnp.mean(wide * wide, axis=1, keepdims=True) + 1e-05)
    weights = lax.all_gather(proj_weight, "dp", axis=0, tiled=True)
    gathered = gather_tensor(inputs).reshape(-1, inputs.shape[1])
    wide_all = gathered.astype(jnp.float32)
    inv_all = lax.rsqrt(jnp.mean(wide_all * wide_all, axis=1, keepdims=True) + 1e-05)
    unit_all = wide_all * inv_all
    positions = (unit_all * norm_gain).astype(jnp.bfloat16)
    length = positions.shape[0]
    streams_rel = jnp.einsum(
        "td,dsc->tsc", positions, weights, preferred_element_type=jnp.float32
    ).astype(jnp.bfloat16)
    streams = jnp.take(
        streams_rel.reshape((-1, rows) + streams_rel.shape[1:]), relative, axis=0
    ).reshape(streams_rel.shape)
    before = passed_along(streams[length - width :], "dp", 1)
    extended = jnp.concatenate([before, streams], axis=0).astype(jnp.float32)
    conv = jnp.zeros(streams.shape, jnp.float32)
    for tap in range(taps):
        conv = conv + filters[:, tap, :] * extended[width - tap : width - tap + length]
    mixed = (conv[:, 0] * conv[:, 1] * conv[:, 2]).astype(jnp.bfloat16)
    grad_out = cotangent.astype(jnp.float32)
    grad_conv = jnp.stack(
        [
            grad_out * conv[:, 1] * conv[:, 2],
            grad_out * conv[:, 0] * conv[:, 2],
            grad_out * conv[:, 0] * conv[:, 1],
        ],
        axis=1,
    )
    after = passed_along(grad_conv[:width], "dp", -1)
    grad_extended = jnp.concatenate([grad_conv, after], axis=0)
    grad_acc = jnp.zeros(streams.shape, jnp.float32)
    for tap in range(taps):
        grad_acc = grad_acc + filters[:, tap, :] * grad_extended[tap : tap + length]
    grad_streams_abs = grad_acc.astype(jnp.bfloat16)
    grad_streams = jnp.take(
        grad_streams_abs.reshape((-1, rows) + grad_streams_abs.shape[1:]), absolute, axis=0
    ).reshape(grad_streams_abs.shape)
    filter_local = jnp.stack(
        [
            jnp.sum(grad_conv * extended[width - tap : width - tap + length], axis=0)
            for tap in range(taps)
        ],
        axis=1,
    )
    grad_filters = butterfly_sum(filter_local, "dp")
    normed_terms = jnp.einsum(
        "tsc,dsc->td", grad_streams, weights, preferred_element_type=jnp.float32
    ).astype(jnp.bfloat16)
    gain_local = jnp.sum(normed_terms.astype(jnp.float32) * unit_all, axis=0)
    grad_normed = scatter_tensor(normed_terms.reshape(-1, rows, normed_terms.shape[1]))
    weight_terms = jnp.einsum(
        "td,tsc->dsc", positions, grad_streams, preferred_element_type=jnp.float32
    )
    grad_proj = lax.psum_scatter(
        weight_terms.astype(jnp.bfloat16), "dp", scatter_dimension=0, tiled=True
    )
    grad_gain = butterfly_sum(butterfly_sum(gain_local, "dp"), "tensor")
    scaled = norm_gain * grad_normed
    grad_inputs = inv_rms * (
        scaled - wide * inv_rms * inv_rms * jnp.mean(scaled * wide, axis=1, keepdims=True)
    )
    return (mixed, grad_inputs.astype(jnp.bfloat16), grad_proj, grad_filters, grad_gain)


def solution(mesh):
    return jax.shard_map(
        body,
        mesh=mesh,
        in_specs=(
            P(("dp", "tensor"), None),
            P(),
            P("dp", None, "tensor"),
            P(None, None, "tensor"),
            P("dp", "tensor"),
        ),
        out_specs=(
            P("dp", "tensor"),
            P(("dp", "tensor"), None),
            P("dp", None, "tensor"),
            P(None, None, "tensor"),
            P(),
        ),
        check_vma=False,
    )
```

```python
import jax
import jax.numpy as jnp
from jax import lax
from jax.sharding import PartitionSpec as P

TENSOR_SPLIT = (2, 4)
DP_SPLIT = (4, 4, 2)


def passed_along(shard, axis, by):
    size = lax.axis_size(axis)
    pairs = [(i, i + by) for i in range(size) if 0 <= i + by < size]
    return lax.ppermute(shard, axis, pairs)


def butterfly_sum(value, axis):
    size = lax.axis_size(axis)
    step = 1
    while step < size:
        pairs = [(i, i ^ step) for i in range(size)]
        value = value + lax.ppermute(value, axis, pairs)
        step *= 2
    return value


def digits(index, split):
    out = []
    for size in reversed(split):
        out.append(index % size)
        index = index // size
    return out[::-1]


def number(parts, split):
    index = 0
    for part, size in zip(parts, split):
        index = index * size + part
    return index


def mover(axis, split, field):
    def move(value, by):
        pairs = []
        for i in range(lax.axis_size(axis)):
            parts = digits(i, split)
            parts[field] = (parts[field] + by) % split[field]
            pairs.append((i, number(parts, split)))
        return lax.ppermute(value, axis, pairs)

    return move


def halves(value, axis):
    cut = value.shape[axis] // 2
    return (
        lax.slice_in_dim(value, 0, cut, axis=axis),
        lax.slice_in_dim(value, cut, value.shape[axis], axis=axis),
    )


def ring_gather(own, move, axis):
    from_left = move(own, 1)
    from_right = move(own, -1)
    far = jnp.concatenate(
        [move(halves(from_left, axis)[0], 1), move(halves(from_right, axis)[1], -1)], axis=axis
    )
    return [own, from_right, far, from_left]


def ring_scatter(shard, move, axis):
    first_far, second_far = halves(shard[2], axis)
    got_left = move(first_far.astype(jnp.bfloat16), 1).astype(jnp.float32)
    got_right = move(second_far.astype(jnp.bfloat16), -1).astype(jnp.float32)
    first, second = halves(shard[1], axis)
    send_right = jnp.concatenate([first + got_left, second], axis=axis)
    first, second = halves(shard[3], axis)
    send_left = jnp.concatenate([first, second + got_right], axis=axis)
    return (
        shard[0]
        + move(send_right.astype(jnp.bfloat16), 1).astype(jnp.float32)
        + move(send_left.astype(jnp.bfloat16), -1).astype(jnp.float32)
    )


def slot_tables(axis, split):
    me = digits(lax.axis_index(axis), split)
    total = 1
    for size in split:
        total *= size
    r = digits(jnp.arange(total, dtype=jnp.int32), split)
    absolute = number([(m + d) % s for m, d, s in zip(me, r, split)], split)
    relative = number([(d - m) % s for m, d, s in zip(me, r, split)], split)
    return absolute, relative


def gather_tensor(own):
    along_x = mover("tensor", TENSOR_SPLIT, 1)
    across_z = mover("tensor", TENSOR_SPLIT, 0)
    partner = across_z(own, 1)
    return jnp.stack(ring_gather(own, along_x, 0) + ring_gather(partner, along_x, 0))


def scatter_tensor(blocks):
    along_x = mover("tensor", TENSOR_SPLIT, 1)
    across_z = mover("tensor", TENSOR_SPLIT, 0)
    wide = blocks.astype(jnp.float32).reshape(TENSOR_SPLIT + blocks.shape[1:])
    column = ring_scatter([wide[:, k] for k in range(TENSOR_SPLIT[1])], along_x, 1)
    return column[0] + across_z(column[1].astype(jnp.bfloat16), 1).astype(jnp.float32)


def gather_dp(own):
    along_y = mover("dp", DP_SPLIT, 0)
    along_h = mover("dp", DP_SPLIT, 1)
    across_core = mover("dp", DP_SPLIT, 2)
    column = jnp.stack(ring_gather(own, along_h, 0))
    grid = jnp.stack(ring_gather(column, along_y, 1))
    both = jnp.stack([grid, across_core(grid, 1)], axis=2)
    return both.reshape((-1,) + own.shape)


def scatter_dp(blocks):
    along_y = mover("dp", DP_SPLIT, 0)
    along_h = mover("dp", DP_SPLIT, 1)
    across_core = mover("dp", DP_SPLIT, 2)
    grid = blocks.reshape(DP_SPLIT + blocks.shape[1:])
    summed = grid[:, :, 0].astype(jnp.float32) + across_core(grid[:, :, 1], 1).astype(jnp.float32)
    column = ring_scatter([summed[k] for k in range(DP_SPLIT[0])], along_y, 1)
    return ring_scatter([column[k] for k in range(DP_SPLIT[1])], along_h, 0)


def body(inputs, norm_gain, proj_weight, filters, cotangent):
    taps = filters.shape[1]
    width = taps - 1
    rows = inputs.shape[0]
    t_absolute, t_relative = slot_tables("tensor", TENSOR_SPLIT)
    d_absolute, d_relative = slot_tables("dp", DP_SPLIT)
    wide = inputs.astype(jnp.float32)
    inv_rms = lax.rsqrt(jnp.mean(wide * wide, axis=1, keepdims=True) + 1e-05)
    weights = jnp.take(gather_dp(proj_weight), d_relative, axis=0).reshape(
        (-1,) + proj_weight.shape[1:]
    )
    gathered = gather_tensor(inputs).reshape(-1, inputs.shape[1])
    wide_all = gathered.astype(jnp.float32)
    inv_all = lax.rsqrt(jnp.mean(wide_all * wide_all, axis=1, keepdims=True) + 1e-05)
    unit_all = wide_all * inv_all
    positions = (unit_all * norm_gain).astype(jnp.bfloat16)
    length = positions.shape[0]
    streams_rel = jnp.einsum(
        "td,dsc->tsc", positions, weights, preferred_element_type=jnp.float32
    ).astype(jnp.bfloat16)
    streams = jnp.take(
        streams_rel.reshape((-1, rows) + streams_rel.shape[1:]), t_relative, axis=0
    ).reshape(streams_rel.shape)
    before = passed_along(streams[length - width :], "dp", 1)
    extended = jnp.concatenate([before, streams], axis=0).astype(jnp.float32)
    conv = jnp.zeros(streams.shape, jnp.float32)
    for tap in range(taps):
        conv = conv + filters[:, tap, :] * extended[width - tap : width - tap + length]
    mixed = (conv[:, 0] * conv[:, 1] * conv[:, 2]).astype(jnp.bfloat16)
    grad_out = cotangent.astype(jnp.float32)
    grad_conv = jnp.stack(
        [
            grad_out * conv[:, 1] * conv[:, 2],
            grad_out * conv[:, 0] * conv[:, 2],
            grad_out * conv[:, 0] * conv[:, 1],
        ],
        axis=1,
    )
    after = passed_along(grad_conv[:width], "dp", -1)
    grad_extended = jnp.concatenate([grad_conv, after], axis=0)
    grad_acc = jnp.zeros(streams.shape, jnp.float32)
    for tap in range(taps):
        grad_acc = grad_acc + filters[:, tap, :] * grad_extended[tap : tap + length]
    grad_streams_abs = grad_acc.astype(jnp.bfloat16)
    grad_streams = jnp.take(
        grad_streams_abs.reshape((-1, rows) + grad_streams_abs.shape[1:]), t_absolute, axis=0
    ).reshape(grad_streams_abs.shape)
    filter_local = jnp.stack(
        [
            jnp.sum(grad_conv * extended[width - tap : width - tap + length], axis=0)
            for tap in range(taps)
        ],
        axis=1,
    )
    normed_terms = jnp.einsum(
        "tsc,dsc->td", grad_streams, weights, preferred_element_type=jnp.float32
    ).astype(jnp.bfloat16)
    gain_local = jnp.sum(normed_terms.astype(jnp.float32) * unit_all, axis=0)
    grad_normed = scatter_tensor(normed_terms.reshape(-1, rows, normed_terms.shape[1]))
    weight_terms = jnp.einsum(
        "td,tsc->dsc", positions, grad_streams, preferred_element_type=jnp.float32
    ).astype(jnp.bfloat16)
    block = proj_weight.shape[0]
    weight_blocks = jnp.take(
        weight_terms.reshape((-1, block) + weight_terms.shape[1:]), d_absolute, axis=0
    )
    grad_proj = scatter_dp(weight_blocks).astype(jnp.bfloat16)
    joined = butterfly_sum(jnp.concatenate([filter_local.reshape(-1), gain_local]), "dp")
    grad_filters = joined[: filter_local.size].reshape(filter_local.shape)
    grad_gain = butterfly_sum(joined[filter_local.size :], "tensor")
    scaled = norm_gain * grad_normed
    grad_inputs = inv_rms * (
        scaled - wide * inv_rms * inv_rms * jnp.mean(scaled * wide, axis=1, keepdims=True)
    )
    return (mixed, grad_inputs.astype(jnp.bfloat16), grad_proj, grad_filters, grad_gain)


def solution(mesh):
    return jax.shard_map(
        body,
        mesh=mesh,
        in_specs=(
            P(("dp", "tensor"), None),
            P(),
            P("dp", None, "tensor"),
            P(None, None, "tensor"),
            P("dp", "tensor"),
        ),
        out_specs=(
            P("dp", "tensor"),
            P(("dp", "tensor"), None),
            P("dp", None, "tensor"),
            P(None, None, "tensor"),
            P(),
        ),
        check_vma=False,
    )
```

```python
import jax
import jax.numpy as jnp
from jax import lax
from jax.sharding import PartitionSpec as P

TENSOR_SPLIT = (2, 4)
DP_SPLIT = (4, 4, 2)
CHANNEL_PIECES = 2


def passed_along(shard, axis, by):
    size = lax.axis_size(axis)
    pairs = [(i, i + by) for i in range(size) if 0 <= i + by < size]
    return lax.ppermute(shard, axis, pairs)


def butterfly_sum(value, axis):
    size = lax.axis_size(axis)
    step = 1
    while step < size:
        pairs = [(i, i ^ step) for i in range(size)]
        value = value + lax.ppermute(value, axis, pairs)
        step *= 2
    return value


def digits(index, split):
    out = []
    for size in reversed(split):
        out.append(index % size)
        index = index // size
    return out[::-1]


def number(parts, split):
    index = 0
    for part, size in zip(parts, split):
        index = index * size + part
    return index


def mover(axis, split, field):
    def move(value, by):
        pairs = []
        for i in range(lax.axis_size(axis)):
            parts = digits(i, split)
            parts[field] = (parts[field] + by) % split[field]
            pairs.append((i, number(parts, split)))
        return lax.ppermute(value, axis, pairs)

    return move


def halves(value, axis):
    cut = value.shape[axis] // 2
    return (
        lax.slice_in_dim(value, 0, cut, axis=axis),
        lax.slice_in_dim(value, cut, value.shape[axis], axis=axis),
    )


def ring_gather(own, move, axis):
    from_left = move(own, 1)
    from_right = move(own, -1)
    far = jnp.concatenate(
        [move(halves(from_left, axis)[0], 1), move(halves(from_right, axis)[1], -1)], axis=axis
    )
    return [own, from_right, far, from_left]


def ring_scatter(shard, move, axis):
    first_far, second_far = halves(shard[2], axis)
    got_left = move(first_far.astype(jnp.bfloat16), 1).astype(jnp.float32)
    got_right = move(second_far.astype(jnp.bfloat16), -1).astype(jnp.float32)
    first, second = halves(shard[1], axis)
    send_right = jnp.concatenate([first + got_left, second], axis=axis)
    first, second = halves(shard[3], axis)
    send_left = jnp.concatenate([first, second + got_right], axis=axis)
    return (
        shard[0]
        + move(send_right.astype(jnp.bfloat16), 1).astype(jnp.float32)
        + move(send_left.astype(jnp.bfloat16), -1).astype(jnp.float32)
    )


def slot_tables(axis, split):
    me = digits(lax.axis_index(axis), split)
    total = 1
    for size in split:
        total *= size
    r = digits(jnp.arange(total, dtype=jnp.int32), split)
    absolute = number([(m + d) % s for m, d, s in zip(me, r, split)], split)
    relative = number([(d - m) % s for m, d, s in zip(me, r, split)], split)
    return absolute, relative


def gather_tensor(own):
    along_x = mover("tensor", TENSOR_SPLIT, 1)
    across_z = mover("tensor", TENSOR_SPLIT, 0)
    partner = across_z(own, 1)
    return jnp.stack(ring_gather(own, along_x, 0) + ring_gather(partner, along_x, 0))


def scatter_tensor(blocks):
    along_x = mover("tensor", TENSOR_SPLIT, 1)
    across_z = mover("tensor", TENSOR_SPLIT, 0)
    wide = blocks.astype(jnp.float32).reshape(TENSOR_SPLIT + blocks.shape[1:])
    column = ring_scatter([wide[:, k] for k in range(TENSOR_SPLIT[1])], along_x, 1)
    return column[0] + across_z(column[1].astype(jnp.bfloat16), 1).astype(jnp.float32)


def body(inputs, norm_gain, proj_weight, filters, cotangent):
    taps = filters.shape[1]
    width = taps - 1
    rows = inputs.shape[0]
    t_absolute, t_relative = slot_tables("tensor", TENSOR_SPLIT)
    wide = inputs.astype(jnp.float32)
    inv_rms = lax.rsqrt(jnp.mean(wide * wide, axis=1, keepdims=True) + 1e-05)
    gathered = gather_tensor(inputs).reshape(-1, inputs.shape[1])
    wide_all = gathered.astype(jnp.float32)
    inv_all = lax.rsqrt(jnp.mean(wide_all * wide_all, axis=1, keepdims=True) + 1e-05)
    unit_all = wide_all * inv_all
    positions = (unit_all * norm_gain).astype(jnp.bfloat16)
    length = positions.shape[0]
    channels = proj_weight.shape[2]
    pieces = CHANNEL_PIECES
    piece = channels // pieces
    mixed_parts, proj_parts, filter_parts = [], [], []
    normed_sum = None
    gate = None
    for k in range(pieces):
        cut = slice(k * piece, (k + 1) * piece)
        weights = lax.all_gather(proj_weight[:, :, cut], "dp", axis=0, tiled=True)
        if gate is not None:
            weights, _ = lax.optimization_barrier((weights, gate))
        taps_k = filters[:, :, cut]
        streams_rel = jnp.einsum(
            "td,dsc->tsc", positions, weights, preferred_element_type=jnp.float32
        ).astype(jnp.bfloat16)
        streams = jnp.take(
            streams_rel.reshape((-1, rows) + streams_rel.shape[1:]), t_relative, axis=0
        ).reshape(streams_rel.shape)
        before = passed_along(streams[length - width :], "dp", 1)
        extended = jnp.concatenate([before, streams], axis=0).astype(jnp.float32)
        conv = jnp.zeros(streams.shape, jnp.float32)
        for tap in range(taps):
            conv = conv + taps_k[:, tap, :] * extended[width - tap : width - tap + length]
        mixed_parts.append((conv[:, 0] * conv[:, 1] * conv[:, 2]).astype(jnp.bfloat16))
        grad_out = cotangent[:, cut].astype(jnp.float32)
        grad_conv = jnp.stack(
            [
                grad_out * conv[:, 1] * conv[:, 2],
                grad_out * conv[:, 0] * conv[:, 2],
                grad_out * conv[:, 0] * conv[:, 1],
            ],
            axis=1,
        )
        after = passed_along(grad_conv[:width], "dp", -1)
        grad_extended = jnp.concatenate([grad_conv, after], axis=0)
        grad_acc = jnp.zeros(streams.shape, jnp.float32)
        for tap in range(taps):
            grad_acc = grad_acc + taps_k[:, tap, :] * grad_extended[tap : tap + length]
        grad_streams_abs = grad_acc.astype(jnp.bfloat16)
        grad_streams = jnp.take(
            grad_streams_abs.reshape((-1, rows) + grad_streams_abs.shape[1:]), t_absolute, axis=0
        ).reshape(grad_streams_abs.shape)
        filter_parts.append(
            jnp.stack(
                [
                    jnp.sum(grad_conv * extended[width - tap : width - tap + length], axis=0)
                    for tap in range(taps)
                ],
                axis=1,
            )
        )
        term = jnp.einsum(
            "tsc,dsc->td", grad_streams, weights, preferred_element_type=jnp.float32
        )
        normed_sum = term if normed_sum is None else normed_sum + term
        weight_terms = jnp.einsum(
            "td,tsc->dsc", positions, grad_streams, preferred_element_type=jnp.float32
        )
        weight_terms = weight_terms.astype(jnp.bfloat16)
        proj_parts.append(
            lax.psum_scatter(weight_terms, "dp", scatter_dimension=0, tiled=True)
        )
        gate = (weight_terms, normed_sum)
    mixed = jnp.concatenate(mixed_parts, axis=1)
    grad_proj = jnp.concatenate(proj_parts, axis=2)
    filter_local = jnp.concatenate(filter_parts, axis=2)
    normed_terms = normed_sum.astype(jnp.bfloat16)
    gain_local = jnp.sum(normed_terms.astype(jnp.float32) * unit_all, axis=0)
    grad_normed = scatter_tensor(normed_terms.reshape(-1, rows, normed_terms.shape[1]))
    joined = butterfly_sum(jnp.concatenate([filter_local.reshape(-1), gain_local]), "dp")
    grad_filters = joined[: filter_local.size].reshape(filter_local.shape)
    grad_gain = butterfly_sum(joined[filter_local.size :], "tensor")
    scaled = norm_gain * grad_normed
    grad_inputs = inv_rms * (
        scaled - wide * inv_rms * inv_rms * jnp.mean(scaled * wide, axis=1, keepdims=True)
    )
    return (mixed, grad_inputs.astype(jnp.bfloat16), grad_proj, grad_filters, grad_gain)


def solution(mesh):
    return jax.shard_map(
        body,
        mesh=mesh,
        in_specs=(
            P(("dp", "tensor"), None),
            P(),
            P("dp", None, "tensor"),
            P(None, None, "tensor"),
            P("dp", "tensor"),
        ),
        out_specs=(
            P("dp", "tensor"),
            P(("dp", "tensor"), None),
            P("dp", None, "tensor"),
            P(None, None, "tensor"),
            P(),
        ),
        check_vma=False,
    )
```

```python
import jax
import jax.numpy as jnp
from jax import lax
from jax.sharding import PartitionSpec as P

TENSOR_SPLIT = (2, 4)
DP_SPLIT = (4, 4, 2)


def passed_along(shard, axis, by):
    size = lax.axis_size(axis)
    pairs = [(i, i + by) for i in range(size) if 0 <= i + by < size]
    return lax.ppermute(shard, axis, pairs)


def butterfly_sum(value, axis):
    size = lax.axis_size(axis)
    step = 1
    while step < size:
        pairs = [(i, i ^ step) for i in range(size)]
        value = value + lax.ppermute(value, axis, pairs)
        step *= 2
    return value


def digits(index, split):
    out = []
    for size in reversed(split):
        out.append(index % size)
        index = index // size
    return out[::-1]


def number(parts, split):
    index = 0
    for part, size in zip(parts, split):
        index = index * size + part
    return index


def mover(axis, split, field):
    def move(value, by):
        pairs = []
        for i in range(lax.axis_size(axis)):
            parts = digits(i, split)
            parts[field] = (parts[field] + by) % split[field]
            pairs.append((i, number(parts, split)))
        return lax.ppermute(value, axis, pairs)

    return move


def halves(value, axis):
    cut = value.shape[axis] // 2
    return (
        lax.slice_in_dim(value, 0, cut, axis=axis),
        lax.slice_in_dim(value, cut, value.shape[axis], axis=axis),
    )


def ring_gather(own, move, axis):
    from_left = move(own, 1)
    from_right = move(own, -1)
    far = jnp.concatenate(
        [move(halves(from_left, axis)[0], 1), move(halves(from_right, axis)[1], -1)], axis=axis
    )
    return [own, from_right, far, from_left]


def ring_scatter(shard, move, axis):
    first_far, second_far = halves(shard[2], axis)
    got_left = move(first_far.astype(jnp.bfloat16), 1).astype(jnp.float32)
    got_right = move(second_far.astype(jnp.bfloat16), -1).astype(jnp.float32)
    first, second = halves(shard[1], axis)
    send_right = jnp.concatenate([first + got_left, second], axis=axis)
    first, second = halves(shard[3], axis)
    send_left = jnp.concatenate([first, second + got_right], axis=axis)
    return (
        shard[0]
        + move(send_right.astype(jnp.bfloat16), 1).astype(jnp.float32)
        + move(send_left.astype(jnp.bfloat16), -1).astype(jnp.float32)
    )


def slot_tables(axis, split):
    me = digits(lax.axis_index(axis), split)
    total = 1
    for size in split:
        total *= size
    r = digits(jnp.arange(total, dtype=jnp.int32), split)
    absolute = number([(m + d) % s for m, d, s in zip(me, r, split)], split)
    relative = number([(d - m) % s for m, d, s in zip(me, r, split)], split)
    return absolute, relative


def gather_tensor(own):
    along_x = mover("tensor", TENSOR_SPLIT, 1)
    across_z = mover("tensor", TENSOR_SPLIT, 0)
    partner = across_z(own, 1)
    return jnp.stack(ring_gather(own, along_x, 0) + ring_gather(partner, along_x, 0))


def scatter_dp(blocks):
    along_y = mover("dp", DP_SPLIT, 0)
    along_h = mover("dp", DP_SPLIT, 1)
    across_core = mover("dp", DP_SPLIT, 2)
    grid = blocks.reshape(DP_SPLIT + blocks.shape[1:])
    summed = grid[:, :, 0].astype(jnp.float32) + across_core(grid[:, :, 1], 1).astype(jnp.float32)
    column = ring_scatter([summed[k] for k in range(DP_SPLIT[0])], along_y, 1)
    return ring_scatter([column[k] for k in range(DP_SPLIT[1])], along_h, 0)


def body(inputs, norm_gain, proj_weight, filters, cotangent):
    taps = filters.shape[1]
    width = taps - 1
    rows = inputs.shape[0]
    t_absolute, t_relative = slot_tables("tensor", TENSOR_SPLIT)
    d_absolute, _ = slot_tables("dp", DP_SPLIT)
    wide = inputs.astype(jnp.float32)
    inv_rms = lax.rsqrt(jnp.mean(wide * wide, axis=1, keepdims=True) + 1e-05)
    weights = lax.all_gather(proj_weight, "dp", axis=0, tiled=True)
    gathered = gather_tensor(inputs).reshape(-1, inputs.shape[1])
    wide_all = gathered.astype(jnp.float32)
    inv_all = lax.rsqrt(jnp.mean(wide_all * wide_all, axis=1, keepdims=True) + 1e-05)
    unit_all = wide_all * inv_all
    positions = (unit_all * norm_gain).astype(jnp.bfloat16)
    length = positions.shape[0]
    streams_rel = jnp.einsum(
        "td,dsc->tsc", positions, weights, preferred_element_type=jnp.float32
    ).astype(jnp.bfloat16)
    streams = jnp.take(
        streams_rel.reshape((-1, rows) + streams_rel.shape[1:]), t_relative, axis=0
    ).reshape(streams_rel.shape)
    before = passed_along(streams[length - width :], "dp", 1)
    extended = jnp.concatenate([before, streams], axis=0).astype(jnp.float32)
    conv = jnp.zeros(streams.shape, jnp.float32)
    for tap in range(taps):
        conv = conv + filters[:, tap, :] * extended[width - tap : width - tap + length]
    mixed = (conv[:, 0] * conv[:, 1] * conv[:, 2]).astype(jnp.bfloat16)
    grad_out = cotangent.astype(jnp.float32)
    grad_conv = jnp.stack(
        [
            grad_out * conv[:, 1] * conv[:, 2],
            grad_out * conv[:, 0] * conv[:, 2],
            grad_out * conv[:, 0] * conv[:, 1],
        ],
        axis=1,
    )
    after = passed_along(grad_conv[:width], "dp", -1)
    grad_extended = jnp.concatenate([grad_conv, after], axis=0)
    grad_acc = jnp.zeros(streams.shape, jnp.float32)
    for tap in range(taps):
        grad_acc = grad_acc + filters[:, tap, :] * grad_extended[tap : tap + length]
    grad_streams_abs = grad_acc.astype(jnp.bfloat16)
    grad_streams = jnp.take(
        grad_streams_abs.reshape((-1, rows) + grad_streams_abs.shape[1:]), t_absolute, axis=0
    ).reshape(grad_streams_abs.shape)
    filter_local = jnp.stack(
        [
            jnp.sum(grad_conv * extended[width - tap : width - tap + length], axis=0)
            for tap in range(taps)
        ],
        axis=1,
    )
    normed_terms = jnp.einsum(
        "tsc,dsc->td", grad_streams, weights, preferred_element_type=jnp.float32
    ).astype(jnp.bfloat16)
    gain_local = jnp.sum(normed_terms.astype(jnp.float32) * unit_all, axis=0)
    normed_blocks = jnp.take(
        normed_terms.reshape(-1, rows, normed_terms.shape[1]), t_relative, axis=0
    ).reshape(normed_terms.shape)
    grad_normed = lax.psum_scatter(
        normed_blocks, "tensor", scatter_dimension=0, tiled=True
    ).astype(jnp.float32)
    weight_terms = jnp.einsum(
        "td,tsc->dsc", positions, grad_streams, preferred_element_type=jnp.float32
    ).astype(jnp.bfloat16)
    block = proj_weight.shape[0]
    weight_blocks = jnp.take(
        weight_terms.reshape((-1, block) + weight_terms.shape[1:]), d_absolute, axis=0
    )
    grad_proj = scatter_dp(weight_blocks).astype(jnp.bfloat16)
    joined = butterfly_sum(jnp.concatenate([filter_local.reshape(-1), gain_local]), "dp")
    grad_filters = joined[: filter_local.size].reshape(filter_local.shape)
    grad_gain = butterfly_sum(joined[filter_local.size :], "tensor")
    scaled = norm_gain * grad_normed
    grad_inputs = inv_rms * (
        scaled - wide * inv_rms * inv_rms * jnp.mean(scaled * wide, axis=1, keepdims=True)
    )
    return (mixed, grad_inputs.astype(jnp.bfloat16), grad_proj, grad_filters, grad_gain)


def solution(mesh):
    return jax.shard_map(
        body,
        mesh=mesh,
        in_specs=(
            P(("dp", "tensor"), None),
            P(),
            P("dp", None, "tensor"),
            P(None, None, "tensor"),
            P("dp", "tensor"),
        ),
        out_specs=(
            P("dp", "tensor"),
            P(("dp", "tensor"), None),
            P("dp", None, "tensor"),
            P(None, None, "tensor"),
            P(),
        ),
        check_vma=False,
    )
```

```python
import jax
import jax.numpy as jnp
from jax import lax
from jax.sharding import PartitionSpec as P

TENSOR_SPLIT = (2, 4)
DP_SPLIT = (4, 4, 2)


def passed_along(shard, axis, by):
    size = lax.axis_size(axis)
    pairs = [(i, i + by) for i in range(size) if 0 <= i + by < size]
    return lax.ppermute(shard, axis, pairs)


def butterfly_sum(value, axis):
    size = lax.axis_size(axis)
    step = 1
    while step < size:
        pairs = [(i, i ^ step) for i in range(size)]
        value = value + lax.ppermute(value, axis, pairs)
        step *= 2
    return value


def digits(index, split):
    out = []
    for size in reversed(split):
        out.append(index % size)
        index = index // size
    return out[::-1]


def number(parts, split):
    index = 0
    for part, size in zip(parts, split):
        index = index * size + part
    return index


def mover(axis, split, field):
    def move(value, by):
        pairs = []
        for i in range(lax.axis_size(axis)):
            parts = digits(i, split)
            parts[field] = (parts[field] + by) % split[field]
            pairs.append((i, number(parts, split)))
        return lax.ppermute(value, axis, pairs)

    return move


def halves(value, axis):
    cut = value.shape[axis] // 2
    return (
        lax.slice_in_dim(value, 0, cut, axis=axis),
        lax.slice_in_dim(value, cut, value.shape[axis], axis=axis),
    )


def ring_gather(own, move, axis):
    from_left = move(own, 1)
    from_right = move(own, -1)
    far = jnp.concatenate(
        [move(halves(from_left, axis)[0], 1), move(halves(from_right, axis)[1], -1)], axis=axis
    )
    return [own, from_right, far, from_left]


def ring_scatter(shard, move, axis):
    first_far, second_far = halves(shard[2], axis)
    got_left = move(first_far.astype(jnp.bfloat16), 1).astype(jnp.float32)
    got_right = move(second_far.astype(jnp.bfloat16), -1).astype(jnp.float32)
    first, second = halves(shard[1], axis)
    send_right = jnp.concatenate([first + got_left, second], axis=axis)
    first, second = halves(shard[3], axis)
    send_left = jnp.concatenate([first, second + got_right], axis=axis)
    return (
        shard[0]
        + move(send_right.astype(jnp.bfloat16), 1).astype(jnp.float32)
        + move(send_left.astype(jnp.bfloat16), -1).astype(jnp.float32)
    )


def slot_tables(axis, split):
    me = digits(lax.axis_index(axis), split)
    total = 1
    for size in split:
        total *= size
    r = digits(jnp.arange(total, dtype=jnp.int32), split)
    absolute = number([(m + d) % s for m, d, s in zip(me, r, split)], split)
    relative = number([(d - m) % s for m, d, s in zip(me, r, split)], split)
    return absolute, relative


def gather_tensor(own):
    along_x = mover("tensor", TENSOR_SPLIT, 1)
    across_z = mover("tensor", TENSOR_SPLIT, 0)
    partner = across_z(own, 1)
    return jnp.stack(ring_gather(own, along_x, 0) + ring_gather(partner, along_x, 0))


def scatter_dp(blocks):
    along_y = mover("dp", DP_SPLIT, 0)
    along_h = mover("dp", DP_SPLIT, 1)
    across_core = mover("dp", DP_SPLIT, 2)
    grid = blocks.reshape(DP_SPLIT + blocks.shape[1:])
    summed = grid[:, :, 0].astype(jnp.float32) + across_core(grid[:, :, 1], 1).astype(jnp.float32)
    column = ring_scatter([summed[k] for k in range(DP_SPLIT[0])], along_y, 1)
    return ring_scatter([column[k] for k in range(DP_SPLIT[1])], along_h, 0)


def body(inputs, norm_gain, proj_weight, filters, cotangent):
    taps = filters.shape[1]
    width = taps - 1
    rows = inputs.shape[0]
    _, t_relative = slot_tables("tensor", TENSOR_SPLIT)
    d_absolute, _ = slot_tables("dp", DP_SPLIT)
    wide = inputs.astype(jnp.float32)
    inv_rms = lax.rsqrt(jnp.mean(wide * wide, axis=1, keepdims=True) + 1e-05)
    weights = lax.all_gather(proj_weight, "dp", axis=0, tiled=True)
    gathered = jnp.take(gather_tensor(inputs), t_relative, axis=0).reshape(-1, inputs.shape[1])
    wide_all = gathered.astype(jnp.float32)
    inv_all = lax.rsqrt(jnp.mean(wide_all * wide_all, axis=1, keepdims=True) + 1e-05)
    unit_all = wide_all * inv_all
    positions = (unit_all * norm_gain).astype(jnp.bfloat16)
    length = positions.shape[0]
    streams = jnp.einsum(
        "td,dsc->tsc", positions, weights, preferred_element_type=jnp.float32
    ).astype(jnp.bfloat16)
    before = passed_along(streams[length - width :], "dp", 1)
    extended = jnp.concatenate([before, streams], axis=0).astype(jnp.float32)
    conv = jnp.zeros(streams.shape, jnp.float32)
    for tap in range(taps):
        conv = conv + filters[:, tap, :] * extended[width - tap : width - tap + length]
    mixed = (conv[:, 0] * conv[:, 1] * conv[:, 2]).astype(jnp.bfloat16)
    grad_out = cotangent.astype(jnp.float32)
    grad_conv = jnp.stack(
        [
            grad_out * conv[:, 1] * conv[:, 2],
            grad_out * conv[:, 0] * conv[:, 2],
            grad_out * conv[:, 0] * conv[:, 1],
        ],
        axis=1,
    )
    after = passed_along(grad_conv[:width], "dp", -1)
    grad_extended = jnp.concatenate([grad_conv, after], axis=0)
    grad_acc = jnp.zeros(streams.shape, jnp.float32)
    for tap in range(taps):
        grad_acc = grad_acc + filters[:, tap, :] * grad_extended[tap : tap + length]
    grad_streams = grad_acc.astype(jnp.bfloat16)
    filter_local = jnp.stack(
        [
            jnp.sum(grad_conv * extended[width - tap : width - tap + length], axis=0)
            for tap in range(taps)
        ],
        axis=1,
    )
    normed_terms = jnp.einsum(
        "tsc,dsc->td", grad_streams, weights, preferred_element_type=jnp.float32
    ).astype(jnp.bfloat16)
    gain_local = jnp.sum(normed_terms.astype(jnp.float32) * unit_all, axis=0)
    grad_normed = lax.psum_scatter(
        normed_terms, "tensor", scatter_dimension=0, tiled=True
    ).astype(jnp.float32)
    weight_terms = jnp.einsum(
        "td,tsc->dsc", positions, grad_streams, preferred_element_type=jnp.float32
    ).astype(jnp.bfloat16)
    block = proj_weight.shape[0]
    weight_blocks = jnp.take(
        weight_terms.reshape((-1, block) + weight_terms.shape[1:]), d_absolute, axis=0
    )
    grad_proj = scatter_dp(weight_blocks).astype(jnp.bfloat16)
    joined = butterfly_sum(jnp.concatenate([filter_local.reshape(-1), gain_local]), "dp")
    grad_filters = joined[: filter_local.size].reshape(filter_local.shape)
    grad_gain = butterfly_sum(joined[filter_local.size :], "tensor")
    scaled = norm_gain * grad_normed
    grad_inputs = inv_rms * (
        scaled - wide * inv_rms * inv_rms * jnp.mean(scaled * wide, axis=1, keepdims=True)
    )
    return (mixed, grad_inputs.astype(jnp.bfloat16), grad_proj, grad_filters, grad_gain)


def solution(mesh):
    return jax.shard_map(
        body,
        mesh=mesh,
        in_specs=(
            P(("dp", "tensor"), None),
            P(),
            P("dp", None, "tensor"),
            P(None, None, "tensor"),
            P("dp", "tensor"),
        ),
        out_specs=(
            P("dp", "tensor"),
            P(("dp", "tensor"), None),
            P("dp", None, "tensor"),
            P(None, None, "tensor"),
            P(),
        ),
        check_vma=False,
    )
```

```python
import jax
import jax.numpy as jnp
from jax import lax
from jax.sharding import PartitionSpec as P

TENSOR_SPLIT = (2, 4)
DP_SPLIT = (4, 4, 2)


def passed_along(shard, axis, by):
    size = lax.axis_size(axis)
    pairs = [(i, i + by) for i in range(size) if 0 <= i + by < size]
    return lax.ppermute(shard, axis, pairs)


def butterfly_sum(value, axis):
    size = lax.axis_size(axis)
    step = 1
    while step < size:
        pairs = [(i, i ^ step) for i in range(size)]
        value = value + lax.ppermute(value, axis, pairs)
        step *= 2
    return value


def digits(index, split):
    out = []
    for size in reversed(split):
        out.append(index % size)
        index = index // size
    return out[::-1]


def number(parts, split):
    index = 0
    for part, size in zip(parts, split):
        index = index * size + part
    return index


def mover(axis, split, field):
    def move(value, by):
        pairs = []
        for i in range(lax.axis_size(axis)):
            parts = digits(i, split)
            parts[field] = (parts[field] + by) % split[field]
            pairs.append((i, number(parts, split)))
        return lax.ppermute(value, axis, pairs)

    return move


def halves(value, axis):
    cut = value.shape[axis] // 2
    return (
        lax.slice_in_dim(value, 0, cut, axis=axis),
        lax.slice_in_dim(value, cut, value.shape[axis], axis=axis),
    )


def ring_gather(own, move, axis):
    from_left = move(own, 1)
    from_right = move(own, -1)
    far = jnp.concatenate(
        [move(halves(from_left, axis)[0], 1), move(halves(from_right, axis)[1], -1)], axis=axis
    )
    return [own, from_right, far, from_left]


def ring_scatter(shard, move, axis):
    first_far, second_far = halves(shard[2], axis)
    got_left = move(first_far.astype(jnp.bfloat16), 1).astype(jnp.float32)
    got_right = move(second_far.astype(jnp.bfloat16), -1).astype(jnp.float32)
    first, second = halves(shard[1], axis)
    send_right = jnp.concatenate([first + got_left, second], axis=axis)
    first, second = halves(shard[3], axis)
    send_left = jnp.concatenate([first, second + got_right], axis=axis)
    return (
        shard[0]
        + move(send_right.astype(jnp.bfloat16), 1).astype(jnp.float32)
        + move(send_left.astype(jnp.bfloat16), -1).astype(jnp.float32)
    )


def ring_scatter_direct(shard, move):
    total = shard[0]
    for k, by in ((1, 1), (2, 2), (3, -1)):
        total = total + move(shard[k].astype(jnp.bfloat16), by).astype(jnp.float32)
    return total


def slot_tables(axis, split):
    me = digits(lax.axis_index(axis), split)
    total = 1
    for size in split:
        total *= size
    r = digits(jnp.arange(total, dtype=jnp.int32), split)
    absolute = number([(m + d) % s for m, d, s in zip(me, r, split)], split)
    relative = number([(d - m) % s for m, d, s in zip(me, r, split)], split)
    return absolute, relative


def gather_tensor(own):
    along_x = mover("tensor", TENSOR_SPLIT, 1)
    across_z = mover("tensor", TENSOR_SPLIT, 0)
    partner = across_z(own, 1)
    return jnp.stack(ring_gather(own, along_x, 0) + ring_gather(partner, along_x, 0))


def scatter_dp(blocks):
    along_y = mover("dp", DP_SPLIT, 0)
    along_h = mover("dp", DP_SPLIT, 1)
    across_core = mover("dp", DP_SPLIT, 2)
    grid = blocks.reshape(DP_SPLIT + blocks.shape[1:])
    summed = grid[:, :, 0].astype(jnp.float32) + across_core(grid[:, :, 1], 1).astype(jnp.float32)
    column = ring_scatter_direct([summed[k] for k in range(DP_SPLIT[0])], along_y)
    return ring_scatter_direct([column[k] for k in range(DP_SPLIT[1])], along_h)


def body(inputs, norm_gain, proj_weight, filters, cotangent):
    taps = filters.shape[1]
    width = taps - 1
    rows = inputs.shape[0]
    _, t_relative = slot_tables("tensor", TENSOR_SPLIT)
    d_absolute, _ = slot_tables("dp", DP_SPLIT)
    wide = inputs.astype(jnp.float32)
    inv_rms = lax.rsqrt(jnp.mean(wide * wide, axis=1, keepdims=True) + 1e-05)
    weights = lax.all_gather(proj_weight, "dp", axis=0, tiled=True)
    gathered = jnp.take(gather_tensor(inputs), t_relative, axis=0).reshape(-1, inputs.shape[1])
    wide_all = gathered.astype(jnp.float32)
    inv_all = lax.rsqrt(jnp.mean(wide_all * wide_all, axis=1, keepdims=True) + 1e-05)
    unit_all = wide_all * inv_all
    positions = (unit_all * norm_gain).astype(jnp.bfloat16)
    length = positions.shape[0]
    streams = jnp.einsum(
        "td,dsc->tsc", positions, weights, preferred_element_type=jnp.float32
    ).astype(jnp.bfloat16)
    before = passed_along(streams[length - width :], "dp", 1)
    extended = jnp.concatenate([before, streams], axis=0).astype(jnp.float32)
    conv = jnp.zeros(streams.shape, jnp.float32)
    for tap in range(taps):
        conv = conv + filters[:, tap, :] * extended[width - tap : width - tap + length]
    mixed = (conv[:, 0] * conv[:, 1] * conv[:, 2]).astype(jnp.bfloat16)
    grad_out = cotangent.astype(jnp.float32)
    grad_conv = jnp.stack(
        [
            grad_out * conv[:, 1] * conv[:, 2],
            grad_out * conv[:, 0] * conv[:, 2],
            grad_out * conv[:, 0] * conv[:, 1],
        ],
        axis=1,
    )
    after = passed_along(grad_conv[:width], "dp", -1)
    grad_extended = jnp.concatenate([grad_conv, after], axis=0)
    grad_acc = jnp.zeros(streams.shape, jnp.float32)
    for tap in range(taps):
        grad_acc = grad_acc + filters[:, tap, :] * grad_extended[tap : tap + length]
    grad_streams = grad_acc.astype(jnp.bfloat16)
    filter_local = jnp.stack(
        [
            jnp.sum(grad_conv * extended[width - tap : width - tap + length], axis=0)
            for tap in range(taps)
        ],
        axis=1,
    )
    normed_terms = jnp.einsum(
        "tsc,dsc->td", grad_streams, weights, preferred_element_type=jnp.float32
    ).astype(jnp.bfloat16)
    gain_local = jnp.sum(normed_terms.astype(jnp.float32) * unit_all, axis=0)
    grad_normed = lax.psum_scatter(
        normed_terms, "tensor", scatter_dimension=0, tiled=True
    ).astype(jnp.float32)
    weight_terms = jnp.einsum(
        "td,tsc->dsc", positions, grad_streams, preferred_element_type=jnp.float32
    ).astype(jnp.bfloat16)
    block = proj_weight.shape[0]
    weight_blocks = jnp.take(
        weight_terms.reshape((-1, block) + weight_terms.shape[1:]), d_absolute, axis=0
    )
    grad_proj = scatter_dp(weight_blocks).astype(jnp.bfloat16)
    joined = butterfly_sum(jnp.concatenate([filter_local.reshape(-1), gain_local]), "dp")
    grad_filters = joined[: filter_local.size].reshape(filter_local.shape)
    grad_gain = butterfly_sum(joined[filter_local.size :], "tensor")
    scaled = norm_gain * grad_normed
    grad_inputs = inv_rms * (
        scaled - wide * inv_rms * inv_rms * jnp.mean(scaled * wide, axis=1, keepdims=True)
    )
    return (mixed, grad_inputs.astype(jnp.bfloat16), grad_proj, grad_filters, grad_gain)


def solution(mesh):
    return jax.shard_map(
        body,
        mesh=mesh,
        in_specs=(
            P(("dp", "tensor"), None),
            P(),
            P("dp", None, "tensor"),
            P(None, None, "tensor"),
            P("dp", "tensor"),
        ),
        out_specs=(
            P("dp", "tensor"),
            P(("dp", "tensor"), None),
            P("dp", None, "tensor"),
            P(None, None, "tensor"),
            P(),
        ),
        check_vma=False,
    )
```

```python
import jax
import jax.numpy as jnp
from jax import lax
from jax.sharding import PartitionSpec as P

TENSOR_SPLIT = (2, 4)
DP_SPLIT = (4, 4, 2)


def passed_along(shard, axis, by):
    size = lax.axis_size(axis)
    pairs = [(i, i + by) for i in range(size) if 0 <= i + by < size]
    return lax.ppermute(shard, axis, pairs)


def butterfly_sum(value, axis):
    size = lax.axis_size(axis)
    step = 1
    while step < size:
        pairs = [(i, i ^ step) for i in range(size)]
        value = value + lax.ppermute(value, axis, pairs)
        step *= 2
    return value


def digits(index, split):
    out = []
    for size in reversed(split):
        out.append(index % size)
        index = index // size
    return out[::-1]


def number(parts, split):
    index = 0
    for part, size in zip(parts, split):
        index = index * size + part
    return index


def mover(axis, split, field):
    def move(value, by):
        pairs = []
        for i in range(lax.axis_size(axis)):
            parts = digits(i, split)
            parts[field] = (parts[field] + by) % split[field]
            pairs.append((i, number(parts, split)))
        return lax.ppermute(value, axis, pairs)

    return move


def halves(value, axis):
    cut = value.shape[axis] // 2
    return (
        lax.slice_in_dim(value, 0, cut, axis=axis),
        lax.slice_in_dim(value, cut, value.shape[axis], axis=axis),
    )


def ring_gather(own, move, axis):
    from_left = move(own, 1)
    from_right = move(own, -1)
    far = jnp.concatenate(
        [move(halves(from_left, axis)[0], 1), move(halves(from_right, axis)[1], -1)], axis=axis
    )
    return [own, from_right, far, from_left]


def ring_scatter(shard, move, axis):
    first_far, second_far = halves(shard[2], axis)
    got_left = move(first_far.astype(jnp.bfloat16), 1).astype(jnp.float32)
    got_right = move(second_far.astype(jnp.bfloat16), -1).astype(jnp.float32)
    first, second = halves(shard[1], axis)
    send_right = jnp.concatenate([first + got_left, second], axis=axis)
    first, second = halves(shard[3], axis)
    send_left = jnp.concatenate([first, second + got_right], axis=axis)
    return (
        shard[0]
        + move(send_right.astype(jnp.bfloat16), 1).astype(jnp.float32)
        + move(send_left.astype(jnp.bfloat16), -1).astype(jnp.float32)
    )


def ring_scatter_direct(shard, move):
    total = shard[0]
    for k, by in ((1, 1), (2, 2), (3, -1)):
        total = total + move(shard[k].astype(jnp.bfloat16), by).astype(jnp.float32)
    return total


def slot_tables(axis, split):
    me = digits(lax.axis_index(axis), split)
    total = 1
    for size in split:
        total *= size
    r = digits(jnp.arange(total, dtype=jnp.int32), split)
    absolute = number([(m + d) % s for m, d, s in zip(me, r, split)], split)
    relative = number([(d - m) % s for m, d, s in zip(me, r, split)], split)
    return absolute, relative


def gather_tensor(own):
    along_x = mover("tensor", TENSOR_SPLIT, 1)
    across_z = mover("tensor", TENSOR_SPLIT, 0)
    partner = across_z(own, 1)
    return jnp.stack(ring_gather(own, along_x, 0) + ring_gather(partner, along_x, 0))


def scatter_dp(blocks):
    along_y = mover("dp", DP_SPLIT, 0)
    along_h = mover("dp", DP_SPLIT, 1)
    across_core = mover("dp", DP_SPLIT, 2)
    grid = blocks.reshape(DP_SPLIT + blocks.shape[1:])
    summed = grid[:, :, 0].astype(jnp.float32) + across_core(grid[:, :, 1], 1).astype(jnp.float32)
    column = ring_scatter_direct([summed[k] for k in range(DP_SPLIT[0])], along_y)
    return ring_scatter_direct([column[k] for k in range(DP_SPLIT[1])], along_h)


def body(inputs, norm_gain, proj_weight, filters, cotangent):
    taps = filters.shape[1]
    width = taps - 1
    rows = inputs.shape[0]
    _, t_relative = slot_tables("tensor", TENSOR_SPLIT)
    d_absolute, _ = slot_tables("dp", DP_SPLIT)
    wide = inputs.astype(jnp.float32)
    inv_rms = lax.rsqrt(jnp.mean(wide * wide, axis=1, keepdims=True) + 1e-05)
    weights = lax.all_gather(proj_weight, "dp", axis=0, tiled=True)
    gathered = jnp.take(gather_tensor(inputs), t_relative, axis=0).reshape(-1, inputs.shape[1])
    wide_all = gathered.astype(jnp.float32)
    inv_all = lax.rsqrt(jnp.mean(wide_all * wide_all, axis=1, keepdims=True) + 1e-05)
    unit_all = wide_all * inv_all
    positions = (unit_all * norm_gain).astype(jnp.bfloat16)
    length = positions.shape[0]
    edge_rows = jnp.concatenate(
        [
            passed_along(gathered[length - width :], "dp", 1),
            passed_along(gathered[:width], "dp", -1),
        ],
        axis=0,
    ).astype(jnp.float32)
    edge_inv = lax.rsqrt(jnp.mean(edge_rows * edge_rows, axis=1, keepdims=True) + 1e-05)
    edge_positions = (edge_rows * edge_inv * norm_gain).astype(jnp.bfloat16)
    next_grad_out = passed_along(cotangent[:width], "dp", -1).astype(jnp.float32)
    streams = jnp.einsum(
        "td,dsc->tsc", positions, weights, preferred_element_type=jnp.float32
    ).astype(jnp.bfloat16)
    edge_streams = jnp.einsum(
        "td,dsc->tsc", edge_positions, weights, preferred_element_type=jnp.float32
    ).astype(jnp.bfloat16)
    extended = jnp.concatenate([edge_streams[:width], streams], axis=0).astype(jnp.float32)
    conv = jnp.zeros(streams.shape, jnp.float32)
    for tap in range(taps):
        conv = conv + filters[:, tap, :] * extended[width - tap : width - tap + length]
    mixed = (conv[:, 0] * conv[:, 1] * conv[:, 2]).astype(jnp.bfloat16)
    grad_out = cotangent.astype(jnp.float32)
    grad_conv = jnp.stack(
        [
            grad_out * conv[:, 1] * conv[:, 2],
            grad_out * conv[:, 0] * conv[:, 2],
            grad_out * conv[:, 0] * conv[:, 1],
        ],
        axis=1,
    )
    next_window = jnp.concatenate(
        [streams[length - width :], edge_streams[width:]], axis=0
    ).astype(jnp.float32)
    next_conv = jnp.zeros((width,) + streams.shape[1:], jnp.float32)
    for tap in range(taps):
        next_conv = next_conv + filters[:, tap, :] * next_window[width - tap : 2 * width - tap]
    after = jnp.stack(
        [
            next_grad_out * next_conv[:, 1] * next_conv[:, 2],
            next_grad_out * next_conv[:, 0] * next_conv[:, 2],
            next_grad_out * next_conv[:, 0] * next_conv[:, 1],
        ],
        axis=1,
    )
    grad_extended = jnp.concatenate([grad_conv, after], axis=0)
    grad_acc = jnp.zeros(streams.shape, jnp.float32)
    for tap in range(taps):
        grad_acc = grad_acc + filters[:, tap, :] * grad_extended[tap : tap + length]
    grad_streams = grad_acc.astype(jnp.bfloat16)
    normed_terms = jnp.einsum(
        "tsc,dsc->td", grad_streams, weights, preferred_element_type=jnp.float32
    ).astype(jnp.bfloat16)
    late_conv, late_extended, _ = lax.optimization_barrier((grad_conv, extended, normed_terms))
    filter_local = jnp.stack(
        [
            jnp.sum(late_conv * late_extended[width - tap : width - tap + length], axis=0)
            for tap in range(taps)
        ],
        axis=1,
    )
    gain_local = jnp.sum(normed_terms.astype(jnp.float32) * unit_all, axis=0)
    grad_normed = lax.psum_scatter(
        normed_terms, "tensor", scatter_dimension=0, tiled=True
    ).astype(jnp.float32)
    weight_terms = jnp.einsum(
        "td,tsc->dsc", positions, grad_streams, preferred_element_type=jnp.float32
    ).astype(jnp.bfloat16)
    block = proj_weight.shape[0]
    weight_blocks = jnp.take(
        weight_terms.reshape((-1, block) + weight_terms.shape[1:]), d_absolute, axis=0
    )
    grad_proj = scatter_dp(weight_blocks).astype(jnp.bfloat16)
    joined = butterfly_sum(jnp.concatenate([filter_local.reshape(-1), gain_local]), "dp")
    grad_filters = joined[: filter_local.size].reshape(filter_local.shape)
    grad_gain = butterfly_sum(joined[filter_local.size :], "tensor")
    scaled = norm_gain * grad_normed
    grad_inputs = inv_rms * (
        scaled - wide * inv_rms * inv_rms * jnp.mean(scaled * wide, axis=1, keepdims=True)
    )
    return (mixed, grad_inputs.astype(jnp.bfloat16), grad_proj, grad_filters, grad_gain)


def solution(mesh):
    return jax.shard_map(
        body,
        mesh=mesh,
        in_specs=(
            P(("dp", "tensor"), None),
            P(),
            P("dp", None, "tensor"),
            P(None, None, "tensor"),
            P("dp", "tensor"),
        ),
        out_specs=(
            P("dp", "tensor"),
            P(("dp", "tensor"), None),
            P("dp", None, "tensor"),
            P(None, None, "tensor"),
            P(),
        ),
        check_vma=False,
    )
```

```python
import jax
import jax.numpy as jnp
from jax import lax
from jax.sharding import PartitionSpec as P

TENSOR_SPLIT = (2, 4)
DP_SPLIT = (4, 4, 2)


def passed_along(shard, axis, by):
    size = lax.axis_size(axis)
    pairs = [(i, i + by) for i in range(size) if 0 <= i + by < size]
    return lax.ppermute(shard, axis, pairs)


def butterfly_sum(value, axis):
    size = lax.axis_size(axis)
    step = 1
    while step < size:
        pairs = [(i, i ^ step) for i in range(size)]
        value = value + lax.ppermute(value, axis, pairs)
        step *= 2
    return value


def digits(index, split):
    out = []
    for size in reversed(split):
        out.append(index % size)
        index = index // size
    return out[::-1]


def number(parts, split):
    index = 0
    for part, size in zip(parts, split):
        index = index * size + part
    return index


def mover(axis, split, field):
    def move(value, by):
        pairs = []
        for i in range(lax.axis_size(axis)):
            parts = digits(i, split)
            parts[field] = (parts[field] + by) % split[field]
            pairs.append((i, number(parts, split)))
        return lax.ppermute(value, axis, pairs)

    return move


def halves(value, axis):
    cut = value.shape[axis] // 2
    return (
        lax.slice_in_dim(value, 0, cut, axis=axis),
        lax.slice_in_dim(value, cut, value.shape[axis], axis=axis),
    )


def ring_gather(own, move, axis):
    from_left = move(own, 1)
    from_right = move(own, -1)
    far = jnp.concatenate(
        [move(halves(from_left, axis)[0], 1), move(halves(from_right, axis)[1], -1)], axis=axis
    )
    return [own, from_right, far, from_left]


def ring_scatter(shard, move, axis):
    first_far, second_far = halves(shard[2], axis)
    got_left = move(first_far.astype(jnp.bfloat16), 1).astype(jnp.float32)
    got_right = move(second_far.astype(jnp.bfloat16), -1).astype(jnp.float32)
    first, second = halves(shard[1], axis)
    send_right = jnp.concatenate([first + got_left, second], axis=axis)
    first, second = halves(shard[3], axis)
    send_left = jnp.concatenate([first, second + got_right], axis=axis)
    return (
        shard[0]
        + move(send_right.astype(jnp.bfloat16), 1).astype(jnp.float32)
        + move(send_left.astype(jnp.bfloat16), -1).astype(jnp.float32)
    )


def ring_scatter_direct(shard, move):
    total = shard[0]
    for k, by in ((1, 1), (2, 2), (3, -1)):
        total = total + move(shard[k].astype(jnp.bfloat16), by).astype(jnp.float32)
    return total


def slot_tables(axis, split):
    me = digits(lax.axis_index(axis), split)
    total = 1
    for size in split:
        total *= size
    r = digits(jnp.arange(total, dtype=jnp.int32), split)
    absolute = number([(m + d) % s for m, d, s in zip(me, r, split)], split)
    relative = number([(d - m) % s for m, d, s in zip(me, r, split)], split)
    return absolute, relative


def gather_tensor(own):
    along_x = mover("tensor", TENSOR_SPLIT, 1)
    across_z = mover("tensor", TENSOR_SPLIT, 0)
    partner = across_z(own, 1)
    return jnp.stack(ring_gather(own, along_x, 0) + ring_gather(partner, along_x, 0))


def coded(vec, row):
    hi = vec.astype(jnp.bfloat16)
    lo = (vec - hi.astype(jnp.float32)).astype(jnp.bfloat16)
    width = 1
    for size in row:
        width *= size
    count = -(-2 * vec.shape[0] // width)
    flat = jnp.pad(jnp.concatenate([hi, lo]), (0, count * width - 2 * vec.shape[0]))
    return flat.reshape((count,) + row), hi.astype(jnp.float32) + lo.astype(jnp.float32)


def decoded(rows, length):
    flat = rows.reshape(-1)
    return flat[:length].astype(jnp.float32) + flat[length : 2 * length].astype(jnp.float32)


def with_rows(block, rows):
    flat = block.astype(jnp.bfloat16).reshape((-1,) + rows.shape[1:])
    return jnp.concatenate([flat, rows], axis=0)


def ring_stage(shard, vec, move, place):
    rows, own = coded(vec, shard[0].shape[-2:])
    count = rows.shape[0]
    total = shard[0].astype(jnp.float32)
    held = {0: own}
    for k, by in ((1, 1), (2, 2), (3, -1)):
        got = move(with_rows(shard[k], rows), by)
        total = total + got[:-count].reshape(shard[k].shape).astype(jnp.float32)
        held[(-by) % 4] = decoded(got[-count:], vec.shape[0])
    ordered = jnp.take(jnp.stack([held[r] for r in range(4)]), (jnp.arange(4) - place) % 4, axis=0)
    return total, (ordered[0] + ordered[1]) + (ordered[2] + ordered[3])


def scatter_dp(blocks, vec):
    along_y = mover("dp", DP_SPLIT, 0)
    along_h = mover("dp", DP_SPLIT, 1)
    across_core = mover("dp", DP_SPLIT, 2)
    place = digits(lax.axis_index("dp"), DP_SPLIT)
    grid = blocks.reshape(DP_SPLIT + blocks.shape[1:])
    rows, own = coded(vec, grid.shape[-2:])
    count = rows.shape[0]
    got = across_core(with_rows(grid[:, :, 1], rows), 1)
    summed = grid[:, :, 0].astype(jnp.float32) + got[:-count].reshape(
        grid[:, :, 1].shape
    ).astype(jnp.float32)
    vec = own + decoded(got[-count:], vec.shape[0])
    column, vec = ring_stage(summed, vec, along_y, place[0])
    return ring_stage(column, vec, along_h, place[1])


def body(inputs, norm_gain, proj_weight, filters, cotangent):
    taps = filters.shape[1]
    width = taps - 1
    rows = inputs.shape[0]
    _, t_relative = slot_tables("tensor", TENSOR_SPLIT)
    d_absolute, _ = slot_tables("dp", DP_SPLIT)
    wide = inputs.astype(jnp.float32)
    inv_rms = lax.rsqrt(jnp.mean(wide * wide, axis=1, keepdims=True) + 1e-05)
    weights = lax.all_gather(proj_weight, "dp", axis=0, tiled=True)
    gathered = jnp.take(gather_tensor(inputs), t_relative, axis=0).reshape(-1, inputs.shape[1])
    wide_all = gathered.astype(jnp.float32)
    inv_all = lax.rsqrt(jnp.mean(wide_all * wide_all, axis=1, keepdims=True) + 1e-05)
    unit_all = wide_all * inv_all
    positions = (unit_all * norm_gain).astype(jnp.bfloat16)
    length = positions.shape[0]
    edge_rows = jnp.concatenate(
        [
            passed_along(gathered[length - width :], "dp", 1),
            passed_along(gathered[:width], "dp", -1),
        ],
        axis=0,
    ).astype(jnp.float32)
    edge_inv = lax.rsqrt(jnp.mean(edge_rows * edge_rows, axis=1, keepdims=True) + 1e-05)
    edge_positions = (edge_rows * edge_inv * norm_gain).astype(jnp.bfloat16)
    next_grad_out = passed_along(cotangent[:width], "dp", -1).astype(jnp.float32)
    streams = jnp.einsum(
        "td,dsc->tsc", positions, weights, preferred_element_type=jnp.float32
    ).astype(jnp.bfloat16)
    edge_streams = jnp.einsum(
        "td,dsc->tsc", edge_positions, weights, preferred_element_type=jnp.float32
    ).astype(jnp.bfloat16)
    extended = jnp.concatenate([edge_streams[:width], streams], axis=0).astype(jnp.float32)
    conv = jnp.zeros(streams.shape, jnp.float32)
    for tap in range(taps):
        conv = conv + filters[:, tap, :] * extended[width - tap : width - tap + length]
    mixed = (conv[:, 0] * conv[:, 1] * conv[:, 2]).astype(jnp.bfloat16)
    grad_out = cotangent.astype(jnp.float32)
    grad_conv = jnp.stack(
        [
            grad_out * conv[:, 1] * conv[:, 2],
            grad_out * conv[:, 0] * conv[:, 2],
            grad_out * conv[:, 0] * conv[:, 1],
        ],
        axis=1,
    )
    next_window = jnp.concatenate(
        [streams[length - width :], edge_streams[width:]], axis=0
    ).astype(jnp.float32)
    next_conv = jnp.zeros((width,) + streams.shape[1:], jnp.float32)
    for tap in range(taps):
        next_conv = next_conv + filters[:, tap, :] * next_window[width - tap : 2 * width - tap]
    after = jnp.stack(
        [
            next_grad_out * next_conv[:, 1] * next_conv[:, 2],
            next_grad_out * next_conv[:, 0] * next_conv[:, 2],
            next_grad_out * next_conv[:, 0] * next_conv[:, 1],
        ],
        axis=1,
    )
    grad_extended = jnp.concatenate([grad_conv, after], axis=0)
    grad_acc = jnp.zeros(streams.shape, jnp.float32)
    for tap in range(taps):
        grad_acc = grad_acc + filters[:, tap, :] * grad_extended[tap : tap + length]
    grad_streams = grad_acc.astype(jnp.bfloat16)
    normed_terms = jnp.einsum(
        "tsc,dsc->td", grad_streams, weights, preferred_element_type=jnp.float32
    ).astype(jnp.bfloat16)
    late_conv, late_extended, _ = lax.optimization_barrier((grad_conv, extended, normed_terms))
    filter_local = jnp.stack(
        [
            jnp.sum(late_conv * late_extended[width - tap : width - tap + length], axis=0)
            for tap in range(taps)
        ],
        axis=1,
    )
    gain_local = jnp.sum(normed_terms.astype(jnp.float32) * unit_all, axis=0)
    grad_normed = lax.psum_scatter(
        normed_terms, "tensor", scatter_dimension=0, tiled=True
    ).astype(jnp.float32)
    weight_terms = jnp.einsum(
        "td,tsc->dsc", positions, grad_streams, preferred_element_type=jnp.float32
    ).astype(jnp.bfloat16)
    block = proj_weight.shape[0]
    weight_blocks = jnp.take(
        weight_terms.reshape((-1, block) + weight_terms.shape[1:]), d_absolute, axis=0
    )
    proj_sum, joined = scatter_dp(
        weight_blocks, jnp.concatenate([filter_local.reshape(-1), gain_local])
    )
    grad_proj = proj_sum.astype(jnp.bfloat16)
    grad_filters = joined[: filter_local.size].reshape(filter_local.shape)
    grad_gain = butterfly_sum(joined[filter_local.size :], "tensor")
    scaled = norm_gain * grad_normed
    grad_inputs = inv_rms * (
        scaled - wide * inv_rms * inv_rms * jnp.mean(scaled * wide, axis=1, keepdims=True)
    )
    return (mixed, grad_inputs.astype(jnp.bfloat16), grad_proj, grad_filters, grad_gain)


def solution(mesh):
    return jax.shard_map(
        body,
        mesh=mesh,
        in_specs=(
            P(("dp", "tensor"), None),
            P(),
            P("dp", None, "tensor"),
            P(None, None, "tensor"),
            P("dp", "tensor"),
        ),
        out_specs=(
            P("dp", "tensor"),
            P(("dp", "tensor"), None),
            P("dp", None, "tensor"),
            P(None, None, "tensor"),
            P(),
        ),
        check_vma=False,
    )
```

```python
import jax
import jax.numpy as jnp
from jax import lax
from jax.sharding import PartitionSpec as P

TENSOR_SPLIT = (2, 4)
DP_SPLIT = (4, 4, 2)


def passed_along(shard, axis, by):
    size = lax.axis_size(axis)
    pairs = [(i, i + by) for i in range(size) if 0 <= i + by < size]
    return lax.ppermute(shard, axis, pairs)


def butterfly_sum(value, axis):
    size = lax.axis_size(axis)
    step = 1
    while step < size:
        pairs = [(i, i ^ step) for i in range(size)]
        value = value + lax.ppermute(value, axis, pairs)
        step *= 2
    return value


def digits(index, split):
    out = []
    for size in reversed(split):
        out.append(index % size)
        index = index // size
    return out[::-1]


def number(parts, split):
    index = 0
    for part, size in zip(parts, split):
        index = index * size + part
    return index


def mover(axis, split, field):
    def move(value, by):
        pairs = []
        for i in range(lax.axis_size(axis)):
            parts = digits(i, split)
            parts[field] = (parts[field] + by) % split[field]
            pairs.append((i, number(parts, split)))
        return lax.ppermute(value, axis, pairs)

    return move


def halves(value, axis):
    cut = value.shape[axis] // 2
    return (
        lax.slice_in_dim(value, 0, cut, axis=axis),
        lax.slice_in_dim(value, cut, value.shape[axis], axis=axis),
    )


def ring_gather(own, move, axis):
    from_left = move(own, 1)
    from_right = move(own, -1)
    far = jnp.concatenate(
        [move(halves(from_left, axis)[0], 1), move(halves(from_right, axis)[1], -1)], axis=axis
    )
    return [own, from_right, far, from_left]


def ring_scatter(shard, move, axis):
    first_far, second_far = halves(shard[2], axis)
    got_left = move(first_far.astype(jnp.bfloat16), 1).astype(jnp.float32)
    got_right = move(second_far.astype(jnp.bfloat16), -1).astype(jnp.float32)
    first, second = halves(shard[1], axis)
    send_right = jnp.concatenate([first + got_left, second], axis=axis)
    first, second = halves(shard[3], axis)
    send_left = jnp.concatenate([first, second + got_right], axis=axis)
    return (
        shard[0]
        + move(send_right.astype(jnp.bfloat16), 1).astype(jnp.float32)
        + move(send_left.astype(jnp.bfloat16), -1).astype(jnp.float32)
    )


def ring_scatter_direct(shard, move):
    total = shard[0]
    for k, by in ((1, 1), (2, 2), (3, -1)):
        total = total + move(shard[k].astype(jnp.bfloat16), by).astype(jnp.float32)
    return total


def slot_tables(axis, split):
    me = digits(lax.axis_index(axis), split)
    total = 1
    for size in split:
        total *= size
    r = digits(jnp.arange(total, dtype=jnp.int32), split)
    absolute = number([(m + d) % s for m, d, s in zip(me, r, split)], split)
    relative = number([(d - m) % s for m, d, s in zip(me, r, split)], split)
    return absolute, relative


def gather_tensor(own):
    along_x = mover("tensor", TENSOR_SPLIT, 1)
    across_z = mover("tensor", TENSOR_SPLIT, 0)
    partner = across_z(own, 1)
    return jnp.stack(ring_gather(own, along_x, 0) + ring_gather(partner, along_x, 0))


def scatter_dp(blocks):
    along_y = mover("dp", DP_SPLIT, 0)
    along_h = mover("dp", DP_SPLIT, 1)
    across_core = mover("dp", DP_SPLIT, 2)
    grid = blocks.reshape(DP_SPLIT + blocks.shape[1:])
    summed = grid[:, :, 0].astype(jnp.float32) + across_core(grid[:, :, 1], 1).astype(jnp.float32)
    column = ring_scatter_direct([summed[k] for k in range(DP_SPLIT[0])], along_y)
    return ring_scatter_direct([column[k] for k in range(DP_SPLIT[1])], along_h)


def body(inputs, norm_gain, proj_weight, filters, cotangent):
    taps = filters.shape[1]
    width = taps - 1
    rows = inputs.shape[0]
    _, t_relative = slot_tables("tensor", TENSOR_SPLIT)
    d_absolute, _ = slot_tables("dp", DP_SPLIT)
    wide = inputs.astype(jnp.float32)
    inv_rms = lax.rsqrt(jnp.mean(wide * wide, axis=1, keepdims=True) + 1e-05)
    weights = lax.all_gather(proj_weight, "dp", axis=0, tiled=True)
    gathered = jnp.take(gather_tensor(inputs), t_relative, axis=0).reshape(-1, inputs.shape[1])
    wide_all = gathered.astype(jnp.float32)
    inv_all = lax.rsqrt(jnp.mean(wide_all * wide_all, axis=1, keepdims=True) + 1e-05)
    unit_all = wide_all * inv_all
    positions = (unit_all * norm_gain).astype(jnp.bfloat16)
    length = positions.shape[0]
    edge_rows = jnp.concatenate(
        [
            passed_along(gathered[length - width :], "dp", 1),
            passed_along(gathered[:width], "dp", -1),
        ],
        axis=0,
    ).astype(jnp.float32)
    edge_inv = lax.rsqrt(jnp.mean(edge_rows * edge_rows, axis=1, keepdims=True) + 1e-05)
    edge_positions = (edge_rows * edge_inv * norm_gain).astype(jnp.bfloat16)
    next_grad_out = passed_along(cotangent[:width], "dp", -1).astype(jnp.float32)
    streams = jnp.einsum(
        "td,dsc->tsc", positions, weights, preferred_element_type=jnp.float32
    ).astype(jnp.bfloat16)
    edge_streams = jnp.einsum(
        "td,dsc->tsc", edge_positions, weights, preferred_element_type=jnp.float32
    ).astype(jnp.bfloat16)
    extended = jnp.concatenate([edge_streams[:width], streams], axis=0).astype(jnp.float32)
    conv = jnp.zeros(streams.shape, jnp.float32)
    for tap in range(taps):
        conv = conv + filters[:, tap, :] * extended[width - tap : width - tap + length]
    mixed = (conv[:, 0] * conv[:, 1] * conv[:, 2]).astype(jnp.bfloat16)
    grad_out = cotangent.astype(jnp.float32)
    grad_conv = jnp.stack(
        [
            grad_out * conv[:, 1] * conv[:, 2],
            grad_out * conv[:, 0] * conv[:, 2],
            grad_out * conv[:, 0] * conv[:, 1],
        ],
        axis=1,
    )
    next_window = jnp.concatenate(
        [streams[length - width :], edge_streams[width:]], axis=0
    ).astype(jnp.float32)
    next_conv = jnp.zeros((width,) + streams.shape[1:], jnp.float32)
    for tap in range(taps):
        next_conv = next_conv + filters[:, tap, :] * next_window[width - tap : 2 * width - tap]
    after = jnp.stack(
        [
            next_grad_out * next_conv[:, 1] * next_conv[:, 2],
            next_grad_out * next_conv[:, 0] * next_conv[:, 2],
            next_grad_out * next_conv[:, 0] * next_conv[:, 1],
        ],
        axis=1,
    )
    grad_extended = jnp.concatenate([grad_conv, after], axis=0)
    grad_acc = jnp.zeros(streams.shape, jnp.float32)
    for tap in range(taps):
        grad_acc = grad_acc + filters[:, tap, :] * grad_extended[tap : tap + length]
    grad_streams = grad_acc.astype(jnp.bfloat16)
    normed_terms = jnp.einsum(
        "tsc,dsc->td", grad_streams, weights, preferred_element_type=jnp.float32
    ).astype(jnp.bfloat16)
    late_conv, late_extended, _ = lax.optimization_barrier((grad_conv, extended, normed_terms))
    filter_local = jnp.stack(
        [
            jnp.sum(late_conv * late_extended[width - tap : width - tap + length], axis=0)
            for tap in range(taps)
        ],
        axis=1,
    )
    gain_local = jnp.sum(normed_terms.astype(jnp.float32) * unit_all, axis=0)
    grad_normed = lax.psum_scatter(
        normed_terms, "tensor", scatter_dimension=0, tiled=True
    ).astype(jnp.float32)
    weight_terms = jnp.einsum(
        "td,tsc->dsc", positions, grad_streams, preferred_element_type=jnp.float32
    ).astype(jnp.bfloat16)
    block = proj_weight.shape[0]
    weight_blocks = jnp.take(
        weight_terms.reshape((-1, block) + weight_terms.shape[1:]), d_absolute, axis=0
    )
    grad_proj = scatter_dp(weight_blocks).astype(jnp.bfloat16)
    gain_tensor = butterfly_sum(gain_local, "tensor")
    joined = butterfly_sum(jnp.concatenate([filter_local.reshape(-1), gain_tensor]), "dp")
    grad_filters = joined[: filter_local.size].reshape(filter_local.shape)
    grad_gain = joined[filter_local.size :]
    scaled = norm_gain * grad_normed
    grad_inputs = inv_rms * (
        scaled - wide * inv_rms * inv_rms * jnp.mean(scaled * wide, axis=1, keepdims=True)
    )
    return (mixed, grad_inputs.astype(jnp.bfloat16), grad_proj, grad_filters, grad_gain)


def solution(mesh):
    return jax.shard_map(
        body,
        mesh=mesh,
        in_specs=(
            P(("dp", "tensor"), None),
            P(),
            P("dp", None, "tensor"),
            P(None, None, "tensor"),
            P("dp", "tensor"),
        ),
        out_specs=(
            P("dp", "tensor"),
            P(("dp", "tensor"), None),
            P("dp", None, "tensor"),
            P(None, None, "tensor"),
            P(),
        ),
        check_vma=False,
    )
```

```python
import jax
import jax.numpy as jnp
from jax import lax
from jax.sharding import PartitionSpec as P

TENSOR_SPLIT = (2, 4)
DP_SPLIT = (4, 4, 2)


def passed_along(shard, axis, by):
    size = lax.axis_size(axis)
    pairs = [(i, i + by) for i in range(size) if 0 <= i + by < size]
    return lax.ppermute(shard, axis, pairs)


def butterfly_sum(value, axis):
    size = lax.axis_size(axis)
    step = 1
    while step < size:
        pairs = [(i, i ^ step) for i in range(size)]
        value = value + lax.ppermute(value, axis, pairs)
        step *= 2
    return value


def digits(index, split):
    out = []
    for size in reversed(split):
        out.append(index % size)
        index = index // size
    return out[::-1]


def number(parts, split):
    index = 0
    for part, size in zip(parts, split):
        index = index * size + part
    return index


def mover(axis, split, field):
    def move(value, by):
        pairs = []
        for i in range(lax.axis_size(axis)):
            parts = digits(i, split)
            parts[field] = (parts[field] + by) % split[field]
            pairs.append((i, number(parts, split)))
        return lax.ppermute(value, axis, pairs)

    return move


def halves(value, axis):
    cut = value.shape[axis] // 2
    return (
        lax.slice_in_dim(value, 0, cut, axis=axis),
        lax.slice_in_dim(value, cut, value.shape[axis], axis=axis),
    )


def ring_gather(own, move, axis):
    from_left = move(own, 1)
    from_right = move(own, -1)
    far = jnp.concatenate(
        [move(halves(from_left, axis)[0], 1), move(halves(from_right, axis)[1], -1)], axis=axis
    )
    return [own, from_right, far, from_left]


def ring_scatter(shard, move, axis):
    first_far, second_far = halves(shard[2], axis)
    got_left = move(first_far.astype(jnp.bfloat16), 1).astype(jnp.float32)
    got_right = move(second_far.astype(jnp.bfloat16), -1).astype(jnp.float32)
    first, second = halves(shard[1], axis)
    send_right = jnp.concatenate([first + got_left, second], axis=axis)
    first, second = halves(shard[3], axis)
    send_left = jnp.concatenate([first, second + got_right], axis=axis)
    return (
        shard[0]
        + move(send_right.astype(jnp.bfloat16), 1).astype(jnp.float32)
        + move(send_left.astype(jnp.bfloat16), -1).astype(jnp.float32)
    )


def ring_scatter_direct(shard, move):
    total = shard[0]
    for k, by in ((1, 1), (2, 2), (3, -1)):
        total = total + move(shard[k].astype(jnp.bfloat16), by).astype(jnp.float32)
    return total


def slot_tables(axis, split):
    me = digits(lax.axis_index(axis), split)
    total = 1
    for size in split:
        total *= size
    r = digits(jnp.arange(total, dtype=jnp.int32), split)
    absolute = number([(m + d) % s for m, d, s in zip(me, r, split)], split)
    relative = number([(d - m) % s for m, d, s in zip(me, r, split)], split)
    return absolute, relative


def gather_tensor(own):
    along_x = mover("tensor", TENSOR_SPLIT, 1)
    across_z = mover("tensor", TENSOR_SPLIT, 0)
    partner = across_z(own, 1)
    return jnp.stack(ring_gather(own, along_x, 0) + ring_gather(partner, along_x, 0))


def scatter_dp(blocks):
    along_y = mover("dp", DP_SPLIT, 0)
    along_h = mover("dp", DP_SPLIT, 1)
    across_core = mover("dp", DP_SPLIT, 2)
    grid = blocks.reshape(DP_SPLIT + blocks.shape[1:])
    summed = grid[:, :, 0].astype(jnp.float32) + across_core(grid[:, :, 1], 1).astype(jnp.float32)
    column = ring_scatter_direct([summed[k] for k in range(DP_SPLIT[0])], along_y)
    return ring_scatter_direct([column[k] for k in range(DP_SPLIT[1])], along_h)


def body(inputs, norm_gain, proj_weight, filters, cotangent):
    taps = filters.shape[1]
    width = taps - 1
    rows = inputs.shape[0]
    _, t_relative = slot_tables("tensor", TENSOR_SPLIT)
    d_absolute, _ = slot_tables("dp", DP_SPLIT)
    wide = inputs.astype(jnp.float32)
    inv_rms = lax.rsqrt(jnp.mean(wide * wide, axis=1, keepdims=True) + 1e-05)
    weights = lax.all_gather(proj_weight, "dp", axis=0, tiled=True)
    gathered = jnp.take(gather_tensor(inputs), t_relative, axis=0).reshape(-1, inputs.shape[1])
    wide_all = gathered.astype(jnp.float32)
    inv_all = lax.rsqrt(jnp.mean(wide_all * wide_all, axis=1, keepdims=True) + 1e-05)
    unit_all = wide_all * inv_all
    positions = (unit_all * norm_gain).astype(jnp.bfloat16)
    length = positions.shape[0]
    edge_rows = jnp.concatenate(
        [
            passed_along(gathered[length - width :], "dp", 1),
            passed_along(gathered[:width], "dp", -1),
        ],
        axis=0,
    ).astype(jnp.float32)
    edge_inv = lax.rsqrt(jnp.mean(edge_rows * edge_rows, axis=1, keepdims=True) + 1e-05)
    edge_positions = (edge_rows * edge_inv * norm_gain).astype(jnp.bfloat16)
    next_grad_out = passed_along(cotangent[:width], "dp", -1).astype(jnp.float32)
    streams = jnp.einsum(
        "td,dsc->tsc", positions, weights, preferred_element_type=jnp.float32
    ).astype(jnp.bfloat16)
    edge_streams = jnp.einsum(
        "td,dsc->tsc", edge_positions, weights, preferred_element_type=jnp.float32
    ).astype(jnp.bfloat16)
    extended = jnp.concatenate([edge_streams[:width], streams], axis=0).astype(jnp.float32)
    conv = jnp.zeros(streams.shape, jnp.float32)
    for tap in range(taps):
        conv = conv + filters[:, tap, :] * extended[width - tap : width - tap + length]
    mixed = (conv[:, 0] * conv[:, 1] * conv[:, 2]).astype(jnp.bfloat16)
    grad_out = cotangent.astype(jnp.float32)
    grad_conv = jnp.stack(
        [
            grad_out * conv[:, 1] * conv[:, 2],
            grad_out * conv[:, 0] * conv[:, 2],
            grad_out * conv[:, 0] * conv[:, 1],
        ],
        axis=1,
    )
    next_window = jnp.concatenate(
        [streams[length - width :], edge_streams[width:]], axis=0
    ).astype(jnp.float32)
    next_conv = jnp.zeros((width,) + streams.shape[1:], jnp.float32)
    for tap in range(taps):
        next_conv = next_conv + filters[:, tap, :] * next_window[width - tap : 2 * width - tap]
    after = jnp.stack(
        [
            next_grad_out * next_conv[:, 1] * next_conv[:, 2],
            next_grad_out * next_conv[:, 0] * next_conv[:, 2],
            next_grad_out * next_conv[:, 0] * next_conv[:, 1],
        ],
        axis=1,
    )
    grad_extended = jnp.concatenate([grad_conv, after], axis=0)
    grad_acc = jnp.zeros(streams.shape, jnp.float32)
    for tap in range(taps):
        grad_acc = grad_acc + filters[:, tap, :] * grad_extended[tap : tap + length]
    grad_streams = grad_acc.astype(jnp.bfloat16)
    weight_terms = jnp.einsum(
        "td,tsc->dsc", positions, grad_streams, preferred_element_type=jnp.float32
    ).astype(jnp.bfloat16)
    late_streams, _ = lax.optimization_barrier((grad_streams, weight_terms))
    normed_terms = jnp.einsum(
        "tsc,dsc->td", late_streams, weights, preferred_element_type=jnp.float32
    ).astype(jnp.bfloat16)
    late_conv, late_extended, _ = lax.optimization_barrier((grad_conv, extended, normed_terms))
    filter_local = jnp.stack(
        [
            jnp.sum(late_conv * late_extended[width - tap : width - tap + length], axis=0)
            for tap in range(taps)
        ],
        axis=1,
    )
    gain_local = jnp.sum(normed_terms.astype(jnp.float32) * unit_all, axis=0)
    grad_normed = lax.psum_scatter(
        normed_terms, "tensor", scatter_dimension=0, tiled=True
    ).astype(jnp.float32)

    block = proj_weight.shape[0]
    weight_blocks = jnp.take(
        weight_terms.reshape((-1, block) + weight_terms.shape[1:]), d_absolute, axis=0
    )
    grad_proj = scatter_dp(weight_blocks).astype(jnp.bfloat16)
    joined = butterfly_sum(jnp.concatenate([filter_local.reshape(-1), gain_local]), "dp")
    grad_filters = joined[: filter_local.size].reshape(filter_local.shape)
    grad_gain = butterfly_sum(joined[filter_local.size :], "tensor")
    scaled = norm_gain * grad_normed
    grad_inputs = inv_rms * (
        scaled - wide * inv_rms * inv_rms * jnp.mean(scaled * wide, axis=1, keepdims=True)
    )
    return (mixed, grad_inputs.astype(jnp.bfloat16), grad_proj, grad_filters, grad_gain)


def solution(mesh):
    return jax.shard_map(
        body,
        mesh=mesh,
        in_specs=(
            P(("dp", "tensor"), None),
            P(),
            P("dp", None, "tensor"),
            P(None, None, "tensor"),
            P("dp", "tensor"),
        ),
        out_specs=(
            P("dp", "tensor"),
            P(("dp", "tensor"), None),
            P("dp", None, "tensor"),
            P(None, None, "tensor"),
            P(),
        ),
        check_vma=False,
    )
```

```python
import jax
import jax.numpy as jnp
from jax import lax
from jax.sharding import PartitionSpec as P

TENSOR_SPLIT = (2, 4)
DP_SPLIT = (4, 4, 2)


def passed_along(shard, axis, by):
    size = lax.axis_size(axis)
    pairs = [(i, i + by) for i in range(size) if 0 <= i + by < size]
    return lax.ppermute(shard, axis, pairs)


def butterfly_sum(value, axis):
    size = lax.axis_size(axis)
    step = 1
    while step < size:
        pairs = [(i, i ^ step) for i in range(size)]
        value = value + lax.ppermute(value, axis, pairs)
        step *= 2
    return value


def digits(index, split):
    out = []
    for size in reversed(split):
        out.append(index % size)
        index = index // size
    return out[::-1]


def number(parts, split):
    index = 0
    for part, size in zip(parts, split):
        index = index * size + part
    return index


def mover(axis, split, field):
    def move(value, by):
        pairs = []
        for i in range(lax.axis_size(axis)):
            parts = digits(i, split)
            parts[field] = (parts[field] + by) % split[field]
            pairs.append((i, number(parts, split)))
        return lax.ppermute(value, axis, pairs)

    return move


def halves(value, axis):
    cut = value.shape[axis] // 2
    return (
        lax.slice_in_dim(value, 0, cut, axis=axis),
        lax.slice_in_dim(value, cut, value.shape[axis], axis=axis),
    )


def ring_gather(own, move, axis):
    from_left = move(own, 1)
    from_right = move(own, -1)
    far = jnp.concatenate(
        [move(halves(from_left, axis)[0], 1), move(halves(from_right, axis)[1], -1)], axis=axis
    )
    return [own, from_right, far, from_left]


def ring_scatter(shard, move, axis):
    first_far, second_far = halves(shard[2], axis)
    got_left = move(first_far.astype(jnp.bfloat16), 1).astype(jnp.float32)
    got_right = move(second_far.astype(jnp.bfloat16), -1).astype(jnp.float32)
    first, second = halves(shard[1], axis)
    send_right = jnp.concatenate([first + got_left, second], axis=axis)
    first, second = halves(shard[3], axis)
    send_left = jnp.concatenate([first, second + got_right], axis=axis)
    return (
        shard[0]
        + move(send_right.astype(jnp.bfloat16), 1).astype(jnp.float32)
        + move(send_left.astype(jnp.bfloat16), -1).astype(jnp.float32)
    )


def ring_scatter_direct(shard, move):
    total = shard[0]
    for k, by in ((1, 1), (2, 2), (3, -1)):
        total = total + move(shard[k].astype(jnp.bfloat16), by).astype(jnp.float32)
    return total


def slot_tables(axis, split):
    me = digits(lax.axis_index(axis), split)
    total = 1
    for size in split:
        total *= size
    r = digits(jnp.arange(total, dtype=jnp.int32), split)
    absolute = number([(m + d) % s for m, d, s in zip(me, r, split)], split)
    relative = number([(d - m) % s for m, d, s in zip(me, r, split)], split)
    return absolute, relative


def gather_tensor(own):
    along_x = mover("tensor", TENSOR_SPLIT, 1)
    across_z = mover("tensor", TENSOR_SPLIT, 0)
    partner = across_z(own, 1)
    return jnp.stack(ring_gather(own, along_x, 0) + ring_gather(partner, along_x, 0))


def ring_scatter_absolute(shard, move, place):
    size = shard.shape[0]
    total = lax.dynamic_index_in_dim(shard, place, axis=0, keepdims=False).astype(jnp.float32)
    for k, by in ((1, 1), (2, 2), (3, -1)):
        part = lax.dynamic_index_in_dim(shard, (place + k) % size, axis=0, keepdims=False)
        total = total + move(part.astype(jnp.bfloat16), by).astype(jnp.float32)
    return total


def scatter_dp(blocks):
    along_y = mover("dp", DP_SPLIT, 0)
    along_h = mover("dp", DP_SPLIT, 1)
    across_core = mover("dp", DP_SPLIT, 2)
    y, h, c = digits(lax.axis_index("dp"), DP_SPLIT)
    grid = blocks.reshape(DP_SPLIT + blocks.shape[1:])
    keep = lax.dynamic_index_in_dim(grid, c, axis=2, keepdims=False)
    send = lax.dynamic_index_in_dim(grid, 1 - c, axis=2, keepdims=False)
    summed = keep.astype(jnp.float32) + across_core(send, 1).astype(jnp.float32)
    column = ring_scatter_absolute(summed, along_y, y)
    return ring_scatter_absolute(column, along_h, h)


def body(inputs, norm_gain, proj_weight, filters, cotangent):
    taps = filters.shape[1]
    width = taps - 1
    rows = inputs.shape[0]
    _, t_relative = slot_tables("tensor", TENSOR_SPLIT)
    wide = inputs.astype(jnp.float32)
    inv_rms = lax.rsqrt(jnp.mean(wide * wide, axis=1, keepdims=True) + 1e-05)
    weights = lax.all_gather(proj_weight, "dp", axis=0, tiled=True)
    gathered = jnp.take(gather_tensor(inputs), t_relative, axis=0).reshape(-1, inputs.shape[1])
    wide_all = gathered.astype(jnp.float32)
    inv_all = lax.rsqrt(jnp.mean(wide_all * wide_all, axis=1, keepdims=True) + 1e-05)
    unit_all = wide_all * inv_all
    positions = (unit_all * norm_gain).astype(jnp.bfloat16)
    length = positions.shape[0]
    edge_rows = jnp.concatenate(
        [
            passed_along(gathered[length - width :], "dp", 1),
            passed_along(gathered[:width], "dp", -1),
        ],
        axis=0,
    ).astype(jnp.float32)
    edge_inv = lax.rsqrt(jnp.mean(edge_rows * edge_rows, axis=1, keepdims=True) + 1e-05)
    edge_positions = (edge_rows * edge_inv * norm_gain).astype(jnp.bfloat16)
    next_grad_out = passed_along(cotangent[:width], "dp", -1).astype(jnp.float32)
    streams = jnp.einsum(
        "td,dsc->tsc", positions, weights, preferred_element_type=jnp.float32
    ).astype(jnp.bfloat16)
    edge_streams = jnp.einsum(
        "td,dsc->tsc", edge_positions, weights, preferred_element_type=jnp.float32
    ).astype(jnp.bfloat16)
    extended = jnp.concatenate([edge_streams[:width], streams], axis=0).astype(jnp.float32)
    conv = jnp.zeros(streams.shape, jnp.float32)
    for tap in range(taps):
        conv = conv + filters[:, tap, :] * extended[width - tap : width - tap + length]
    mixed = (conv[:, 0] * conv[:, 1] * conv[:, 2]).astype(jnp.bfloat16)
    grad_out = cotangent.astype(jnp.float32)
    grad_conv = jnp.stack(
        [
            grad_out * conv[:, 1] * conv[:, 2],
            grad_out * conv[:, 0] * conv[:, 2],
            grad_out * conv[:, 0] * conv[:, 1],
        ],
        axis=1,
    )
    next_window = jnp.concatenate(
        [streams[length - width :], edge_streams[width:]], axis=0
    ).astype(jnp.float32)
    next_conv = jnp.zeros((width,) + streams.shape[1:], jnp.float32)
    for tap in range(taps):
        next_conv = next_conv + filters[:, tap, :] * next_window[width - tap : 2 * width - tap]
    after = jnp.stack(
        [
            next_grad_out * next_conv[:, 1] * next_conv[:, 2],
            next_grad_out * next_conv[:, 0] * next_conv[:, 2],
            next_grad_out * next_conv[:, 0] * next_conv[:, 1],
        ],
        axis=1,
    )
    grad_extended = jnp.concatenate([grad_conv, after], axis=0)
    grad_acc = jnp.zeros(streams.shape, jnp.float32)
    for tap in range(taps):
        grad_acc = grad_acc + filters[:, tap, :] * grad_extended[tap : tap + length]
    grad_streams = grad_acc.astype(jnp.bfloat16)
    normed_terms = jnp.einsum(
        "tsc,dsc->td", grad_streams, weights, preferred_element_type=jnp.float32
    ).astype(jnp.bfloat16)
    late_conv, late_extended, _ = lax.optimization_barrier((grad_conv, extended, normed_terms))
    filter_local = jnp.stack(
        [
            jnp.sum(late_conv * late_extended[width - tap : width - tap + length], axis=0)
            for tap in range(taps)
        ],
        axis=1,
    )
    gain_local = jnp.sum(normed_terms.astype(jnp.float32) * unit_all, axis=0)
    grad_normed = lax.psum_scatter(
        normed_terms, "tensor", scatter_dimension=0, tiled=True
    ).astype(jnp.float32)
    weight_terms = jnp.einsum(
        "td,tsc->dsc", positions, grad_streams, preferred_element_type=jnp.float32
    ).astype(jnp.bfloat16)
    block = proj_weight.shape[0]
    weight_blocks = weight_terms.reshape((-1, block) + weight_terms.shape[1:])
    grad_proj = scatter_dp(weight_blocks).astype(jnp.bfloat16)
    joined = butterfly_sum(jnp.concatenate([filter_local.reshape(-1), gain_local]), "dp")
    grad_filters = joined[: filter_local.size].reshape(filter_local.shape)
    grad_gain = butterfly_sum(joined[filter_local.size :], "tensor")
    scaled = norm_gain * grad_normed
    grad_inputs = inv_rms * (
        scaled - wide * inv_rms * inv_rms * jnp.mean(scaled * wide, axis=1, keepdims=True)
    )
    return (mixed, grad_inputs.astype(jnp.bfloat16), grad_proj, grad_filters, grad_gain)


def solution(mesh):
    return jax.shard_map(
        body,
        mesh=mesh,
        in_specs=(
            P(("dp", "tensor"), None),
            P(),
            P("dp", None, "tensor"),
            P(None, None, "tensor"),
            P("dp", "tensor"),
        ),
        out_specs=(
            P("dp", "tensor"),
            P(("dp", "tensor"), None),
            P("dp", None, "tensor"),
            P(None, None, "tensor"),
            P(),
        ),
        check_vma=False,
    )
```

```python
import jax
import jax.numpy as jnp
from jax import lax
from jax.sharding import PartitionSpec as P

TENSOR_SPLIT = (2, 4)
DP_SPLIT = (4, 4, 2)


def passed_along(shard, axis, by):
    size = lax.axis_size(axis)
    pairs = [(i, i + by) for i in range(size) if 0 <= i + by < size]
    return lax.ppermute(shard, axis, pairs)


def butterfly_sum(value, axis):
    size = lax.axis_size(axis)
    step = 1
    while step < size:
        pairs = [(i, i ^ step) for i in range(size)]
        value = value + lax.ppermute(value, axis, pairs)
        step *= 2
    return value


def digits(index, split):
    out = []
    for size in reversed(split):
        out.append(index % size)
        index = index // size
    return out[::-1]


def number(parts, split):
    index = 0
    for part, size in zip(parts, split):
        index = index * size + part
    return index


def mover(axis, split, field):
    def move(value, by):
        pairs = []
        for i in range(lax.axis_size(axis)):
            parts = digits(i, split)
            parts[field] = (parts[field] + by) % split[field]
            pairs.append((i, number(parts, split)))
        return lax.ppermute(value, axis, pairs)

    return move


def halves(value, axis):
    cut = value.shape[axis] // 2
    return (
        lax.slice_in_dim(value, 0, cut, axis=axis),
        lax.slice_in_dim(value, cut, value.shape[axis], axis=axis),
    )


def ring_gather(own, move, axis):
    from_left = move(own, 1)
    from_right = move(own, -1)
    far = jnp.concatenate(
        [move(halves(from_left, axis)[0], 1), move(halves(from_right, axis)[1], -1)], axis=axis
    )
    return [own, from_right, far, from_left]


def ring_scatter(shard, move, axis):
    first_far, second_far = halves(shard[2], axis)
    got_left = move(first_far.astype(jnp.bfloat16), 1).astype(jnp.float32)
    got_right = move(second_far.astype(jnp.bfloat16), -1).astype(jnp.float32)
    first, second = halves(shard[1], axis)
    send_right = jnp.concatenate([first + got_left, second], axis=axis)
    first, second = halves(shard[3], axis)
    send_left = jnp.concatenate([first, second + got_right], axis=axis)
    return (
        shard[0]
        + move(send_right.astype(jnp.bfloat16), 1).astype(jnp.float32)
        + move(send_left.astype(jnp.bfloat16), -1).astype(jnp.float32)
    )


def ring_scatter_direct(shard, move):
    total = shard[0]
    for k, by in ((1, 1), (2, 2), (3, -1)):
        total = total + move(shard[k].astype(jnp.bfloat16), by).astype(jnp.float32)
    return total


def slot_tables(axis, split):
    me = digits(lax.axis_index(axis), split)
    total = 1
    for size in split:
        total *= size
    r = digits(jnp.arange(total, dtype=jnp.int32), split)
    absolute = number([(m + d) % s for m, d, s in zip(me, r, split)], split)
    relative = number([(d - m) % s for m, d, s in zip(me, r, split)], split)
    return absolute, relative


def gather_tensor(own):
    along_x = mover("tensor", TENSOR_SPLIT, 1)
    across_z = mover("tensor", TENSOR_SPLIT, 0)
    partner = across_z(own, 1)
    return jnp.stack(ring_gather(own, along_x, 0) + ring_gather(partner, along_x, 0))


def ring_scatter_absolute(shard, move, place):
    size = shard.shape[0]
    total = lax.dynamic_index_in_dim(shard, place, axis=0, keepdims=False).astype(jnp.float32)
    for k, by in ((1, 1), (2, 2), (3, -1)):
        part = lax.dynamic_index_in_dim(shard, (place + k) % size, axis=0, keepdims=False)
        total = total + move(part.astype(jnp.bfloat16), by).astype(jnp.float32)
    return total


def scatter_dp(blocks):
    along_y = mover("dp", DP_SPLIT, 0)
    along_h = mover("dp", DP_SPLIT, 1)
    across_core = mover("dp", DP_SPLIT, 2)
    y, h, c = digits(lax.axis_index("dp"), DP_SPLIT)
    grid = blocks.reshape(DP_SPLIT + blocks.shape[1:])
    keep = lax.dynamic_index_in_dim(grid, c, axis=2, keepdims=False)
    send = lax.dynamic_index_in_dim(grid, 1 - c, axis=2, keepdims=False)
    summed = keep.astype(jnp.float32) + across_core(send, 1).astype(jnp.float32)
    column = ring_scatter_absolute(summed, along_y, y)
    return ring_scatter_absolute(column, along_h, h)


def body(inputs, norm_gain, proj_weight, filters, cotangent):
    taps = filters.shape[1]
    width = taps - 1
    rows = inputs.shape[0]
    _, t_relative = slot_tables("tensor", TENSOR_SPLIT)
    wide = inputs.astype(jnp.float32)
    inv_rms = lax.rsqrt(jnp.mean(wide * wide, axis=1, keepdims=True) + 1e-05)
    weights = lax.all_gather(proj_weight, "dp", axis=0, tiled=True)
    gathered = jnp.take(gather_tensor(inputs), t_relative, axis=0).reshape(-1, inputs.shape[1])
    wide_all = gathered.astype(jnp.float32)
    inv_all = lax.rsqrt(jnp.mean(wide_all * wide_all, axis=1, keepdims=True) + 1e-05)
    unit_all = wide_all * inv_all
    positions = (unit_all * norm_gain).astype(jnp.bfloat16)
    length = positions.shape[0]
    edge_rows = jnp.concatenate(
        [
            passed_along(gathered[length - width :], "dp", 1),
            passed_along(gathered[:width], "dp", -1),
        ],
        axis=0,
    ).astype(jnp.float32)
    edge_inv = lax.rsqrt(jnp.mean(edge_rows * edge_rows, axis=1, keepdims=True) + 1e-05)
    edge_positions = (edge_rows * edge_inv * norm_gain).astype(jnp.bfloat16)
    next_grad_out = passed_along(cotangent[:width], "dp", -1).astype(jnp.float32)
    streams = jnp.einsum(
        "td,dsc->tsc", positions, weights, preferred_element_type=jnp.float32
    ).astype(jnp.bfloat16)
    edge_streams = jnp.einsum(
        "td,dsc->tsc", edge_positions, weights, preferred_element_type=jnp.float32
    ).astype(jnp.bfloat16)
    extended = jnp.concatenate([edge_streams[:width], streams], axis=0).astype(jnp.float32)
    conv = jnp.zeros(streams.shape, jnp.float32)
    for tap in range(taps):
        conv = conv + filters[:, tap, :] * extended[width - tap : width - tap + length]
    mixed = (conv[:, 0] * conv[:, 1] * conv[:, 2]).astype(jnp.bfloat16)
    grad_out = cotangent.astype(jnp.float32)
    grad_conv = jnp.stack(
        [
            grad_out * conv[:, 1] * conv[:, 2],
            grad_out * conv[:, 0] * conv[:, 2],
            grad_out * conv[:, 0] * conv[:, 1],
        ],
        axis=1,
    )
    next_window = jnp.concatenate(
        [streams[length - width :], edge_streams[width:]], axis=0
    ).astype(jnp.float32)
    next_conv = jnp.zeros((width,) + streams.shape[1:], jnp.float32)
    for tap in range(taps):
        next_conv = next_conv + filters[:, tap, :] * next_window[width - tap : 2 * width - tap]
    after = jnp.stack(
        [
            next_grad_out * next_conv[:, 1] * next_conv[:, 2],
            next_grad_out * next_conv[:, 0] * next_conv[:, 2],
            next_grad_out * next_conv[:, 0] * next_conv[:, 1],
        ],
        axis=1,
    )
    grad_extended = jnp.concatenate([grad_conv, after], axis=0)
    grad_acc = jnp.zeros(streams.shape, jnp.float32)
    for tap in range(taps):
        grad_acc = grad_acc + filters[:, tap, :] * grad_extended[tap : tap + length]
    grad_streams = grad_acc.astype(jnp.bfloat16)
    filter_local = jnp.stack(
        [
            jnp.sum(grad_conv * extended[width - tap : width - tap + length], axis=0)
            for tap in range(taps)
        ],
        axis=1,
    )
    early_streams, _ = lax.optimization_barrier((grad_streams, filter_local))
    normed_terms = jnp.einsum(
        "tsc,dsc->td", early_streams, weights, preferred_element_type=jnp.float32
    ).astype(jnp.bfloat16)
    gain_local = jnp.sum(normed_terms.astype(jnp.float32) * unit_all, axis=0)
    grad_normed = lax.psum_scatter(
        normed_terms, "tensor", scatter_dimension=0, tiled=True
    ).astype(jnp.float32)
    weight_terms = jnp.einsum(
        "td,tsc->dsc", positions, grad_streams, preferred_element_type=jnp.float32
    ).astype(jnp.bfloat16)
    block = proj_weight.shape[0]
    weight_blocks = weight_terms.reshape((-1, block) + weight_terms.shape[1:])
    grad_proj = scatter_dp(weight_blocks).astype(jnp.bfloat16)
    joined = butterfly_sum(jnp.concatenate([filter_local.reshape(-1), gain_local]), "dp")
    grad_filters = joined[: filter_local.size].reshape(filter_local.shape)
    grad_gain = butterfly_sum(joined[filter_local.size :], "tensor")
    scaled = norm_gain * grad_normed
    grad_inputs = inv_rms * (
        scaled - wide * inv_rms * inv_rms * jnp.mean(scaled * wide, axis=1, keepdims=True)
    )
    return (mixed, grad_inputs.astype(jnp.bfloat16), grad_proj, grad_filters, grad_gain)


def solution(mesh):
    return jax.shard_map(
        body,
        mesh=mesh,
        in_specs=(
            P(("dp", "tensor"), None),
            P(),
            P("dp", None, "tensor"),
            P(None, None, "tensor"),
            P("dp", "tensor"),
        ),
        out_specs=(
            P("dp", "tensor"),
            P(("dp", "tensor"), None),
            P("dp", None, "tensor"),
            P(None, None, "tensor"),
            P(),
        ),
        check_vma=False,
    )
```

```python
import jax
import jax.numpy as jnp
from jax import lax
from jax.sharding import PartitionSpec as P

TENSOR_SPLIT = (2, 4)
DP_SPLIT = (4, 4, 2)


def passed_along(shard, axis, by):
    size = lax.axis_size(axis)
    pairs = [(i, i + by) for i in range(size) if 0 <= i + by < size]
    return lax.ppermute(shard, axis, pairs)


def butterfly_sum(value, axis):
    size = lax.axis_size(axis)
    step = 1
    while step < size:
        pairs = [(i, i ^ step) for i in range(size)]
        value = value + lax.ppermute(value, axis, pairs)
        step *= 2
    return value


def digits(index, split):
    out = []
    for size in reversed(split):
        out.append(index % size)
        index = index // size
    return out[::-1]


def number(parts, split):
    index = 0
    for part, size in zip(parts, split):
        index = index * size + part
    return index


def mover(axis, split, field):
    def move(value, by):
        pairs = []
        for i in range(lax.axis_size(axis)):
            parts = digits(i, split)
            parts[field] = (parts[field] + by) % split[field]
            pairs.append((i, number(parts, split)))
        return lax.ppermute(value, axis, pairs)

    return move


def halves(value, axis):
    cut = value.shape[axis] // 2
    return (
        lax.slice_in_dim(value, 0, cut, axis=axis),
        lax.slice_in_dim(value, cut, value.shape[axis], axis=axis),
    )


def ring_gather(own, move, axis):
    from_left = move(own, 1)
    from_right = move(own, -1)
    far = jnp.concatenate(
        [move(halves(from_left, axis)[0], 1), move(halves(from_right, axis)[1], -1)], axis=axis
    )
    return [own, from_right, far, from_left]


def ring_scatter(shard, move, axis):
    first_far, second_far = halves(shard[2], axis)
    got_left = move(first_far.astype(jnp.bfloat16), 1).astype(jnp.float32)
    got_right = move(second_far.astype(jnp.bfloat16), -1).astype(jnp.float32)
    first, second = halves(shard[1], axis)
    send_right = jnp.concatenate([first + got_left, second], axis=axis)
    first, second = halves(shard[3], axis)
    send_left = jnp.concatenate([first, second + got_right], axis=axis)
    return (
        shard[0]
        + move(send_right.astype(jnp.bfloat16), 1).astype(jnp.float32)
        + move(send_left.astype(jnp.bfloat16), -1).astype(jnp.float32)
    )


def ring_scatter_direct(shard, move):
    total = shard[0]
    for k, by in ((1, 1), (2, 2), (3, -1)):
        total = total + move(shard[k].astype(jnp.bfloat16), by).astype(jnp.float32)
    return total


def slot_tables(axis, split):
    me = digits(lax.axis_index(axis), split)
    total = 1
    for size in split:
        total *= size
    r = digits(jnp.arange(total, dtype=jnp.int32), split)
    absolute = number([(m + d) % s for m, d, s in zip(me, r, split)], split)
    relative = number([(d - m) % s for m, d, s in zip(me, r, split)], split)
    return absolute, relative


def gather_tensor(own):
    along_x = mover("tensor", TENSOR_SPLIT, 1)
    across_z = mover("tensor", TENSOR_SPLIT, 0)
    partner = across_z(own, 1)
    return jnp.stack(ring_gather(own, along_x, 0) + ring_gather(partner, along_x, 0))


def ring_scatter_absolute(shard, move, place):
    size = shard.shape[0]
    total = lax.dynamic_index_in_dim(shard, place, axis=0, keepdims=False).astype(jnp.float32)
    for k, by in ((1, 1), (2, 2), (3, -1)):
        part = lax.dynamic_index_in_dim(shard, (place + k) % size, axis=0, keepdims=False)
        total = total + move(part.astype(jnp.bfloat16), by).astype(jnp.float32)
    return total


def scatter_dp(blocks):
    along_y = mover("dp", DP_SPLIT, 0)
    along_h = mover("dp", DP_SPLIT, 1)
    across_core = mover("dp", DP_SPLIT, 2)
    y, h, c = digits(lax.axis_index("dp"), DP_SPLIT)
    grid = blocks.reshape(DP_SPLIT + blocks.shape[1:])
    keep = lax.dynamic_index_in_dim(grid, c, axis=2, keepdims=False)
    send = lax.dynamic_index_in_dim(grid, 1 - c, axis=2, keepdims=False)
    summed = keep.astype(jnp.float32) + across_core(send, 1).astype(jnp.float32)
    column = ring_scatter_absolute(summed, along_y, y)
    return ring_scatter_absolute(column, along_h, h)


def body(inputs, norm_gain, proj_weight, filters, cotangent):
    taps = filters.shape[1]
    width = taps - 1
    rows = inputs.shape[0]
    _, t_relative = slot_tables("tensor", TENSOR_SPLIT)
    wide = inputs.astype(jnp.float32)
    inv_rms = lax.rsqrt(jnp.mean(wide * wide, axis=1, keepdims=True) + 1e-05)
    weights = lax.all_gather(proj_weight, "dp", axis=0, tiled=True)
    gathered = jnp.take(gather_tensor(inputs), t_relative, axis=0).reshape(-1, inputs.shape[1])
    wide_all = gathered.astype(jnp.float32)
    inv_all = lax.rsqrt(jnp.mean(wide_all * wide_all, axis=1, keepdims=True) + 1e-05)
    unit_all = wide_all * inv_all
    positions = (unit_all * norm_gain).astype(jnp.bfloat16)
    length = positions.shape[0]
    edge_rows = jnp.concatenate(
        [
            passed_along(gathered[length - width :], "dp", 1),
            passed_along(gathered[:width], "dp", -1),
        ],
        axis=0,
    ).astype(jnp.float32)
    edge_inv = lax.rsqrt(jnp.mean(edge_rows * edge_rows, axis=1, keepdims=True) + 1e-05)
    edge_positions = (edge_rows * edge_inv * norm_gain).astype(jnp.bfloat16)
    next_grad_out = passed_along(cotangent[:width], "dp", -1).astype(jnp.float32)
    streams = jnp.einsum(
        "td,dsc->tsc", positions, weights, preferred_element_type=jnp.float32
    ).astype(jnp.bfloat16)
    edge_streams = jnp.einsum(
        "td,dsc->tsc", edge_positions, weights, preferred_element_type=jnp.float32
    ).astype(jnp.bfloat16)
    extended = jnp.concatenate([edge_streams[:width], streams], axis=0).astype(jnp.float32)
    conv = jnp.zeros(streams.shape, jnp.float32)
    for tap in range(taps):
        conv = conv + filters[:, tap, :] * extended[width - tap : width - tap + length]
    mixed = (conv[:, 0] * conv[:, 1] * conv[:, 2]).astype(jnp.bfloat16)
    grad_out = cotangent.astype(jnp.float32)
    grad_conv = jnp.stack(
        [
            grad_out * conv[:, 1] * conv[:, 2],
            grad_out * conv[:, 0] * conv[:, 2],
            grad_out * conv[:, 0] * conv[:, 1],
        ],
        axis=1,
    )
    next_window = jnp.concatenate(
        [streams[length - width :], edge_streams[width:]], axis=0
    ).astype(jnp.float32)
    next_conv = jnp.zeros((width,) + streams.shape[1:], jnp.float32)
    for tap in range(taps):
        next_conv = next_conv + filters[:, tap, :] * next_window[width - tap : 2 * width - tap]
    after = jnp.stack(
        [
            next_grad_out * next_conv[:, 1] * next_conv[:, 2],
            next_grad_out * next_conv[:, 0] * next_conv[:, 2],
            next_grad_out * next_conv[:, 0] * next_conv[:, 1],
        ],
        axis=1,
    )
    grad_extended = jnp.concatenate([grad_conv, after], axis=0)
    grad_acc = jnp.zeros(streams.shape, jnp.float32)
    for tap in range(taps):
        grad_acc = grad_acc + filters[:, tap, :] * grad_extended[tap : tap + length]
    grad_streams = grad_acc.astype(jnp.bfloat16)
    weight_terms = jnp.einsum(
        "td,tsc->dsc", positions, grad_streams, preferred_element_type=jnp.float32
    ).astype(jnp.bfloat16)
    late_streams, _ = lax.optimization_barrier((grad_streams, weight_terms))
    normed_terms = jnp.einsum(
        "tsc,dsc->td", late_streams, weights, preferred_element_type=jnp.float32
    ).astype(jnp.bfloat16)
    late_conv, late_extended, _ = lax.optimization_barrier((grad_conv, extended, normed_terms))
    filter_local = jnp.stack(
        [
            jnp.sum(late_conv * late_extended[width - tap : width - tap + length], axis=0)
            for tap in range(taps)
        ],
        axis=1,
    )
    gain_local = jnp.sum(normed_terms.astype(jnp.float32) * unit_all, axis=0)
    grad_normed = lax.psum_scatter(
        normed_terms, "tensor", scatter_dimension=0, tiled=True
    ).astype(jnp.float32)

    block = proj_weight.shape[0]
    weight_blocks = weight_terms.reshape((-1, block) + weight_terms.shape[1:])
    grad_proj = scatter_dp(weight_blocks).astype(jnp.bfloat16)
    joined = butterfly_sum(jnp.concatenate([filter_local.reshape(-1), gain_local]), "dp")
    grad_filters = joined[: filter_local.size].reshape(filter_local.shape)
    grad_gain = butterfly_sum(joined[filter_local.size :], "tensor")
    scaled = norm_gain * grad_normed
    grad_inputs = inv_rms * (
        scaled - wide * inv_rms * inv_rms * jnp.mean(scaled * wide, axis=1, keepdims=True)
    )
    return (mixed, grad_inputs.astype(jnp.bfloat16), grad_proj, grad_filters, grad_gain)


def solution(mesh):
    return jax.shard_map(
        body,
        mesh=mesh,
        in_specs=(
            P(("dp", "tensor"), None),
            P(),
            P("dp", None, "tensor"),
            P(None, None, "tensor"),
            P("dp", "tensor"),
        ),
        out_specs=(
            P("dp", "tensor"),
            P(("dp", "tensor"), None),
            P("dp", None, "tensor"),
            P(None, None, "tensor"),
            P(),
        ),
        check_vma=False,
    )
```
